512 devices in a mesh: dp: 32 (over z, x), mp: 16 (over y, core).
Axes of the slice: x: 4, y: 8, z: 8, core: 2. Of those that a mesh axis runs over, the one named last changes fastest.
Arguments:
- x_feat: bfloat16 [4096, 4096], P('mp', 'dp'), may hold values from -6 to 6
- grad_out: bfloat16 [4096, 4096], P('mp', 'dp'), may hold values from -6 to 6
- w_gate: bfloat16 [2560, 4096], P('mp'), may hold values from -0.21875 to 0.21875
- w_up: bfloat16 [2560, 4096], P('mp'), may hold values from -0.21875 to 0.21875
- w_down: bfloat16 [2560, 4096], P('mp'), may hold values from -1 to 1
- gate_blocks: int32 [2560, 2], P('mp'), may hold values from 0 to 63, as said below
- up_blocks: int32 [2560, 2], P('mp'), may hold values from 0 to 63, as said below
- down_blocks: int32 [2560, 2], P('mp'), may hold values from 0 to 63, as said below
- up_offsets: int32 [17], replicated, may hold values from 0 to 224, as said below
- down_offsets: int32 [17], replicated, may hold values from 0 to 224, as said below
Outputs:
- out_branch: bfloat16 [4096, 4096], P('mp', 'dp')
- grad_in: bfloat16 [4096, 4096], P('mp', 'dp')
- grad_gate: float32 [2560, 4096], P(('mp', 'dp'))
- grad_up: float32 [2560, 4096], P(('mp', 'dp'))
- grad_down: float32 [2560, 4096], P(('mp', 'dp'))
The draws below stay inside these ranges and needn't reach their ends.
Inputs may be any that keep to these rules, and one draw needn't show every extreme that they name: `up_offsets`: starts at 0 and ends at 224; every inner entry j lies 0 to 3 columns above j * 14, so index j of mp owns between 11 and 17 columns, and some index owns exactly 17. `down_offsets`: starts at 0 and ends at 224; every inner entry j lies 1 to 3 columns below j * 14, so index j of mp owns between 11 and 17 columns, and the last index owns exactly 17. `gate_blocks`: rows of index j of mp are (block row below 64, slot below up_offsets[j + 1] - up_offsets[j]); no pair repeats on one index. `up_blocks`: rows of index j of mp are (block row below 64, slot below up_offsets[j + 1] - up_offsets[j]); no pair repeats on one index. `down_blocks`: rows of index j of mp are (block row below 64, slot below down_offsets[j + 1] - down_offsets[j]); no pair repeats on one index.
All inputs are finite; a program needn't handle non-finite values.
Results may differ from the reference program's by a relative error of at most 0.022.
Values may be sent and summed in bfloat16 or wider, within the bound.
No kernel may reach another device: no remote copies, remote signals or barrier semaphores. Data moves between devices by JAX's collectives and lax.ppermute only.
A program may use at most 128 MiB of HBM per device.

```python
import jax
import jax.numpy as jnp
from jax import lax

BS = 64
D = 4096
HC = 14
NB_DEV = 160
ROWS = 128
TOKENS = 4096
CB = 224
CAP = 17
RB = 64
NNZ = 2560
N_DP = 32
N_MP = 16


def make_up_offsets(key):
    groups = CB // HC
    index = jnp.arange(groups + 1, dtype=jnp.int32)
    shifts = jax.random.randint(jax.random.fold_in(key, 1), (groups + 1,), 0, 4).astype(jnp.int32)
    forced = jax.random.randint(jax.random.fold_in(key, 2), (), 1, groups - 1).astype(jnp.int32)
    shifts = jnp.where(index == forced, 0, shifts)
    shifts = jnp.where(index == forced + 1, 3, shifts)
    shifts = jnp.where((index == 0) | (index == groups), 0, shifts)
    return (index * HC + shifts).astype(jnp.int32)


def make_down_offsets(key):
    groups = CB // HC
    index = jnp.arange(groups + 1, dtype=jnp.int32)
    shifts = jax.random.randint(jax.random.fold_in(key, 1), (groups + 1,), -3, 0).astype(jnp.int32)
    shifts = jnp.where(index == groups - 1, -3, shifts)
    shifts = jnp.where((index == 0) | (index == groups), 0, shifts)
    return (index * HC + shifts).astype(jnp.int32)


def place_blocks(key, offsets):
    groups = CB // HC
    counts = offsets[1:] - offsets[:-1]
    positions_all = CAP * RB
    position = jnp.arange(positions_all, dtype=jnp.int32)

    def one_group(sub_key, count):
        scores = jax.random.randint(sub_key, (positions_all,), 0, 65536) * positions_all + position
        scores = jnp.where(position // RB < count, scores, scores + 1073741824)
        last_low = (count - 1) * RB
        scores = jnp.where((position == last_low) | (position == last_low + RB - 1), -1, scores)
        chosen = jnp.argsort(scores)[:NB_DEV].astype(jnp.int32)
        return jnp.stack([chosen % RB, chosen // RB], axis=1)
    group_keys = jax.random.split(key, groups)
    return jax.vmap(one_group)(group_keys, counts).reshape(groups * NB_DEV, 2).astype(jnp.int32)


def draw_up_offsets(key, part):
    return make_up_offsets(jax.random.fold_in(key, 11))


def draw_down_offsets(key, part):
    return make_down_offsets(jax.random.fold_in(key, 12))


def draw_gate_blocks(key, part):
    return place_blocks(jax.random.fold_in(key, 21), make_up_offsets(jax.random.fold_in(key, 11)))


def draw_up_blocks(key, part):
    return place_blocks(jax.random.fold_in(key, 22), make_up_offsets(jax.random.fold_in(key, 11)))


def draw_down_blocks(key, part):
    return place_blocks(jax.random.fold_in(key, 23), make_down_offsets(jax.random.fold_in(key, 12)))


def shard_levels(key, extent, cuts, smallest, high):
    gain, own = 1.0, jax.random.fold_in(key, 6)
    for dim, parts in cuts:
        draws = jnp.exp(jax.random.uniform(jax.random.fold_in(own, dim), (parts,), jnp.float32, smallest / len(cuts), high / len(cuts)))
        gain = gain * jnp.repeat(draws, extent[dim] // parts).reshape([-1 if axis == dim else 1 for axis in range(len(extent))])
    return gain


def gaussian(stream_key, dims, scale, limit, cuts=(), kind=jnp.bfloat16):
    entries = scale * jax.random.normal(stream_key, dims, jnp.float32)
    if cuts:
        entries = entries * shard_levels(stream_key, dims, cuts, -0.22, 0.18)
    return jnp.clip(entries, -limit, limit).astype(kind)


def setup_inputs(seed: int = 0) -> dict:
    seeds = jax.random.split(jax.random.key(seed), 11)
    x_feat = gaussian(seeds[0], (D, TOKENS), 1.0, 6.0, ((0, 16), (1, 32)))
    grad_out = gaussian(seeds[1], (D, TOKENS), 1.0, 6.0, ((0, 16), (1, 32)))
    w_gate = gaussian(seeds[2], (NNZ, BS * BS), (NB_DEV * BS // HC) ** -0.5, 0.21875, ((0, 16),))
    w_up = gaussian(seeds[3], (NNZ, BS * BS), (NB_DEV * BS // HC) ** -0.5, 0.21875, ((0, 16),))
    w_down = gaussian(seeds[4], (NNZ, BS * BS), (NNZ * BS * BS // (80 * D)) ** -0.5, 1.0, ((0, 16),))
    gate_blocks = draw_gate_blocks(jax.random.fold_in(seeds[10], 71), 0)
    up_blocks = draw_up_blocks(jax.random.fold_in(seeds[10], 71), 0)
    down_blocks = draw_down_blocks(jax.random.fold_in(seeds[10], 71), 0)
    up_offsets = draw_up_offsets(jax.random.fold_in(seeds[10], 71), 0)
    down_offsets = draw_down_offsets(jax.random.fold_in(seeds[10], 71), 0)
    return {"x_feat": x_feat, "grad_out": grad_out, "w_gate": w_gate, "w_up": w_up, "w_down": w_down, "gate_blocks": gate_blocks, "up_blocks": up_blocks, "down_blocks": down_blocks, "up_offsets": up_offsets, "down_offsets": down_offsets}


branch_scale = 1.0 / (80.0 ** 0.5)


def owners_of(offsets, columns):
    bounds = offsets[1:-1]
    owners = jnp.sum((bounds[None, :] <= columns[:, None]).astype(jnp.int32), axis=1).astype(jnp.int32)
    return owners, (columns - jnp.take(offsets, owners)).astype(jnp.int32)


def rounded(values):
    return lax.optimization_barrier(values.astype(jnp.bfloat16)).astype(jnp.float32)


def token_pieces(left_side, right_side):
    left_split = left_side.reshape(NB_DEV, BS, N_DP, ROWS)
    right_split = right_side.reshape(NB_DEV, BS, N_DP, ROWS)
    return jnp.einsum('kiqr,koqr->qkio', left_split, right_split)


def reference(x_feat, grad_out, w_gate, w_up, w_down, gate_blocks, up_blocks, down_blocks, up_offsets, down_offsets):
    token_norm = 1.0 / (float(TOKENS) ** 0.5)
    x_blocks = x_feat.reshape(RB, BS, TOKENS)
    dy_blocks = grad_out.reshape(RB, BS, TOKENS)
    gate_w = w_gate.reshape(N_MP, NB_DEV, BS, BS)
    up_w = w_up.reshape(N_MP, NB_DEV, BS, BS)
    down_w = w_down.reshape(N_MP, NB_DEV, BS, BS)
    gate_list = gate_blocks.reshape(N_MP, NB_DEV, 2)
    up_list = up_blocks.reshape(N_MP, NB_DEV, 2)
    down_list = down_blocks.reshape(N_MP, NB_DEV, 2)
    all_columns = jnp.arange(CB, dtype=jnp.int32)

    def forward_group(inputs):
        gate_part, up_part, gate_rows, up_rows = inputs

        def spread(weights, block_list):
            pieces = jnp.take(x_blocks, block_list[:, 0], axis=0).astype(jnp.float32)
            products = jnp.einsum('kit,kio->kot', pieces, weights.astype(jnp.float32))
            return jax.ops.segment_sum(products, block_list[:, 1], num_segments=CAP)

        return spread(gate_part, gate_rows), spread(up_part, up_rows)

    gate_local, up_local = lax.map(forward_group, (gate_w, up_w, gate_list, up_list))
    up_owner, up_slot = owners_of(up_offsets, all_columns)
    gate_pre = gate_local[up_owner, up_slot]
    up_pre = up_local[up_owner, up_slot]
    sigma = jax.nn.sigmoid(gate_pre)
    gate_silu = gate_pre * sigma
    hidden = (gate_silu * up_pre).astype(jnp.bfloat16)

    def down_step(branch_sum, inputs):
        down_part, down_rows, low_col = inputs
        weights = down_part.astype(jnp.float32)
        hid_pieces = jnp.take(hidden, low_col + down_rows[:, 1], axis=0).astype(jnp.float32)
        products = jnp.einsum('kit,kio->kot', hid_pieces, weights)
        partial_value = jax.ops.segment_sum(products, down_rows[:, 0], num_segments=RB) * branch_scale
        dy_pieces = jnp.take(dy_blocks, down_rows[:, 0], axis=0).astype(jnp.float32)
        backward = jnp.einsum('kot,kio->kit', dy_pieces, weights)
        grad_hid = jax.ops.segment_sum(backward, down_rows[:, 1], num_segments=CAP) * branch_scale
        pieces = rounded(token_pieces(hid_pieces, dy_pieces) * (branch_scale * token_norm))
        return branch_sum + rounded(partial_value), (grad_hid, jnp.sum(pieces, axis=0).reshape(NB_DEV, BS * BS))

    branch_sum, (grad_local, grad_down) = lax.scan(
        down_step, jnp.zeros((RB, BS, TOKENS), jnp.float32), (down_w, down_list, down_offsets[:-1]))
    down_owner, down_slot = owners_of(down_offsets, all_columns)
    grad_hidden = grad_local[down_owner, down_slot].astype(jnp.bfloat16).astype(jnp.float32)
    grad_gate_pre = (grad_hidden * up_pre * sigma * (1.0 + gate_pre * (1.0 - sigma))).astype(jnp.bfloat16)
    grad_up_pre = (grad_hidden * gate_silu).astype(jnp.bfloat16)

    def back_step(input_sum, inputs):
        gate_part, up_part, gate_rows, up_rows, low_col = inputs

        def one_side(weights, block_list, source):
            grad_pieces = jnp.take(source, low_col + block_list[:, 1], axis=0).astype(jnp.float32)
            products = jnp.einsum('kot,kio->kit', grad_pieces, weights.astype(jnp.float32))
            x_pieces = jnp.take(x_blocks, block_list[:, 0], axis=0).astype(jnp.float32)
            pieces = rounded(token_pieces(x_pieces, grad_pieces) * token_norm)
            summed = jax.ops.segment_sum(products, block_list[:, 0], num_segments=RB)
            return summed, jnp.sum(pieces, axis=0).reshape(NB_DEV, BS * BS)

        gate_sum, gate_grad = one_side(gate_part, gate_rows, grad_gate_pre)
        up_sum, up_grad = one_side(up_part, up_rows, grad_up_pre)
        return input_sum + rounded(gate_sum + up_sum), (gate_grad, up_grad)

    input_sum, (grad_gate, grad_up) = lax.scan(
        back_step, jnp.zeros((RB, BS, TOKENS), jnp.float32), (gate_w, up_w, gate_list, up_list, up_offsets[:-1]))
    out_branch = branch_sum.reshape(D, TOKENS).astype(jnp.bfloat16)
    grad_in = input_sum.reshape(D, TOKENS).astype(jnp.bfloat16)
    return (out_branch, grad_in, grad_gate.reshape(NNZ, BS * BS), grad_up.reshape(NNZ, BS * BS),
            grad_down.reshape(NNZ, BS * BS))
```

```python
import math

import jax
import jax.numpy as jnp
from jax import lax
from jax.sharding import PartitionSpec as P

BS = 64
HC = 14


branch_scale = 1.0 / math.sqrt(80.0)


def shifted(value, axis, steps):
    count = lax.axis_size(axis)
    first, last = (max(0, -steps), min(count, count - steps))
    return lax.ppermute(value, axis, [(source, source + steps) for source in range(first, last)])


def segment_total(products, targets, out_count):
    choose = (targets[None, :] == jnp.arange(out_count, dtype=targets.dtype)[:, None]).astype(jnp.float32)
    return jnp.einsum(
        "sk,kor->sor",
        choose,
        products,
        precision=lax.Precision.HIGHEST,
        preferred_element_type=jnp.float32,
    )


def spread_rows(weights, pick_rows, targets, source, out_count):
    blocks = weights.reshape(weights.shape[0], BS, BS)
    pieces = jnp.take(source, pick_rows, axis=0)
    products = jnp.einsum("kir,kio->kor", pieces, blocks, preferred_element_type=jnp.float32)
    return segment_total(products, targets, out_count)


def spread_back(weights, pick_rows, targets, source, out_count):
    blocks = weights.reshape(weights.shape[0], BS, BS)
    pieces = jnp.take(source, pick_rows, axis=0)
    products = jnp.einsum("kor,kio->kir", pieces, blocks, preferred_element_type=jnp.float32)
    return segment_total(products, targets, out_count)


def block_grads(left_side, left_rows, right_side, right_rows, factor):
    first_pick = jnp.take(left_side, left_rows, axis=0)
    second_pick = jnp.take(right_side, right_rows, axis=0)
    products = jnp.einsum(
        "kir,kor->kio", first_pick, second_pick, preferred_element_type=jnp.float32
    )
    return (products * factor).astype(jnp.bfloat16).reshape(products.shape[0], BS * BS)


def reduce_pieces(pieces, groups):
    lanes = 128
    flat = pieces.astype(jnp.float32).reshape(pieces.size // lanes, lanes)
    total = lax.psum_scatter(flat, "dp", scatter_dimension=0, tiled=True)
    return total.reshape(pieces.shape[0] // groups, pieces.shape[1])


def pick_near(own, other, own_low, other_low, use_other, columns, filled, slot_cap):
    stacked = jnp.concatenate([own, other], axis=0)
    position = jnp.where(use_other, slot_cap + columns - other_low, columns - own_low)
    position = jnp.clip(jnp.where(filled, position, 0), 0, 2 * slot_cap - 1)
    picked = jnp.take(stacked, position, axis=0)
    return jnp.where(filled[:, None, None], picked, jnp.zeros_like(picked))


def local(
    x_feat,
    grad_out,
    w_gate,
    w_up,
    w_down,
    gate_blocks,
    up_blocks,
    down_blocks,
    up_offsets,
    down_offsets,
):
    row_count = x_feat.shape[1]
    slot_cap = HC + 3
    groups = lax.axis_size("dp")
    mp_index = lax.axis_index("mp")
    token_norm = 1.0 / math.sqrt(row_count * groups)
    x_full, dy_full = (
        lax.all_gather(x_feat, "mp", axis=0, tiled=True),
        lax.all_gather(grad_out, "mp", axis=0, tiled=True),
    )
    block_rows = x_full.shape[0] // BS
    x_blocks = x_full.reshape(block_rows, BS, row_count)
    dy_blocks = dy_full.reshape(block_rows, BS, row_count)
    gate_pre = spread_rows(w_gate, gate_blocks[:, 0], gate_blocks[:, 1], x_blocks, slot_cap)
    up_pre = spread_rows(w_up, up_blocks[:, 0], up_blocks[:, 1], x_blocks, slot_cap)
    sigma = jax.nn.sigmoid(gate_pre)
    gate_silu = gate_pre * sigma
    hidden = (gate_silu * up_pre).astype(jnp.bfloat16)
    up_prev = jnp.take(up_offsets, jnp.maximum(mp_index - 1, 0))
    up_low = jnp.take(up_offsets, mp_index)
    up_high = jnp.take(up_offsets, mp_index + 1)
    down_low = jnp.take(down_offsets, mp_index)
    down_high = jnp.take(down_offsets, mp_index + 1)
    slot_range = jnp.arange(slot_cap, dtype=jnp.int32)
    lower_hidden = shifted(hidden, "mp", 1)
    down_columns = down_low + slot_range
    hidden_down = pick_near(
        hidden,
        lower_hidden,
        up_low,
        up_prev,
        down_columns < up_low,
        down_columns,
        down_columns < down_high,
        slot_cap,
    )
    branch_part = (
        spread_rows(w_down, down_blocks[:, 1], down_blocks[:, 0], hidden_down, block_rows)
        * branch_scale
    )
    grad_hidden = (
        spread_back(w_down, down_blocks[:, 0], down_blocks[:, 1], dy_blocks, slot_cap)
        * branch_scale
    ).astype(jnp.bfloat16)
    down_piece = block_grads(
        hidden_down, down_blocks[:, 1], dy_blocks, down_blocks[:, 0], branch_scale * token_norm
    )
    upper_grad = shifted(grad_hidden, "mp", -1)
    up_columns = up_low + slot_range
    grad_local = pick_near(
        grad_hidden,
        upper_grad,
        down_low,
        down_high,
        up_columns >= down_high,
        up_columns,
        up_columns < up_high,
        slot_cap,
    )
    grad_hid_f = grad_local.astype(jnp.float32)
    grad_gate_pre = (grad_hid_f * up_pre * sigma * (1.0 + gate_pre * (1.0 - sigma))).astype(
        jnp.bfloat16
    )
    grad_up_pre = (grad_hid_f * gate_silu).astype(jnp.bfloat16)
    input_part = spread_back(
        w_gate, gate_blocks[:, 1], gate_blocks[:, 0], grad_gate_pre, block_rows
    )
    input_part = input_part + spread_back(
        w_up, up_blocks[:, 1], up_blocks[:, 0], grad_up_pre, block_rows
    )
    gate_piece = block_grads(
        x_blocks, gate_blocks[:, 0], grad_gate_pre, gate_blocks[:, 1], token_norm
    )
    up_piece = block_grads(x_blocks, up_blocks[:, 0], grad_up_pre, up_blocks[:, 1], token_norm)
    width_all = block_rows * BS
    branch_sum, input_sum = (
        lax.psum_scatter(
            branch_part.reshape(width_all, row_count).astype(jnp.bfloat16),
            "mp",
            scatter_dimension=0,
            tiled=True,
        ).astype(jnp.float32),
        lax.psum_scatter(
            input_part.reshape(width_all, row_count).astype(jnp.bfloat16),
            "mp",
            scatter_dimension=0,
            tiled=True,
        ).astype(jnp.float32),
    )
    down_total, gate_total, up_total = (
        reduce_pieces(down_piece, groups),
        reduce_pieces(gate_piece, groups),
        reduce_pieces(up_piece, groups),
    )
    return (
        branch_sum.astype(jnp.bfloat16),
        input_sum.astype(jnp.bfloat16),
        gate_total,
        up_total,
        down_total,
    )


def solution(mesh):
    in_specs = (
        P("mp", "dp"),
        P("mp", "dp"),
        P("mp", None),
        P("mp", None),
        P("mp", None),
        P("mp", None),
        P("mp", None),
        P("mp", None),
        P(),
        P(),
    )
    out_specs = (
        P("mp", "dp"),
        P("mp", "dp"),
        P(("mp", "dp"), None),
        P(("mp", "dp"), None),
        P(("mp", "dp"), None),
    )
    return jax.shard_map(local, mesh=mesh, in_specs=in_specs, out_specs=out_specs, check_vma=False)
```

```python
import math

import jax
import jax.numpy as jnp
from jax import lax
from jax.sharding import PartitionSpec as P

BS = 64
HC = 14


branch_scale = 1.0 / math.sqrt(80.0)


def shifted(value, axis, steps):
    count = lax.axis_size(axis)
    first, last = (max(0, -steps), min(count, count - steps))
    return lax.ppermute(value, axis, [(source, source + steps) for source in range(first, last)])


def segment_total(products, targets, out_count):
    choose = (targets[None, :] == jnp.arange(out_count, dtype=targets.dtype)[:, None]).astype(jnp.float32)
    return jnp.einsum(
        "sk,kor->sor",
        choose,
        products,
        precision=lax.Precision.HIGHEST,
        preferred_element_type=jnp.float32,
    )


def spread_rows(weights, pick_rows, targets, source, out_count):
    blocks = weights.reshape(weights.shape[0], BS, BS)
    pieces = jnp.take(source, pick_rows, axis=0)
    products = jnp.einsum("kir,kio->kor", pieces, blocks, preferred_element_type=jnp.float32)
    return segment_total(products, targets, out_count)


def spread_back(weights, pick_rows, targets, source, out_count):
    blocks = weights.reshape(weights.shape[0], BS, BS)
    pieces = jnp.take(source, pick_rows, axis=0)
    products = jnp.einsum("kor,kio->kir", pieces, blocks, preferred_element_type=jnp.float32)
    return segment_total(products, targets, out_count)


def block_grads(left_side, left_rows, right_side, right_rows, factor):
    first_pick = jnp.take(left_side, left_rows, axis=0)
    second_pick = jnp.take(right_side, right_rows, axis=0)
    products = jnp.einsum(
        "kir,kor->kio", first_pick, second_pick, preferred_element_type=jnp.float32
    )
    return (products * factor).astype(jnp.bfloat16).reshape(products.shape[0], BS * BS)


def split_groups(pieces, groups):
    return pieces.reshape(groups, pieces.shape[0] // groups, pieces.shape[1])


def reduce_pieces(pieces, groups):
    received = lax.all_to_all(
        split_groups(pieces, groups), "dp", split_axis=0, concat_axis=0, tiled=True
    )
    return jnp.sum(received, axis=0, dtype=jnp.float32)


def pick_near(own, other, own_low, other_low, use_other, columns, filled, slot_cap):
    stacked = jnp.concatenate([own, other], axis=0)
    position = jnp.where(use_other, slot_cap + columns - other_low, columns - own_low)
    position = jnp.clip(jnp.where(filled, position, 0), 0, 2 * slot_cap - 1)
    picked = jnp.take(stacked, position, axis=0)
    return jnp.where(filled[:, None, None], picked, jnp.zeros_like(picked))


def local(
    x_feat,
    grad_out,
    w_gate,
    w_up,
    w_down,
    gate_blocks,
    up_blocks,
    down_blocks,
    up_offsets,
    down_offsets,
):
    row_count = x_feat.shape[1]
    slot_cap = HC + 3
    groups = lax.axis_size("dp")
    mp_index = lax.axis_index("mp")
    token_norm = 1.0 / math.sqrt(row_count * groups)
    x_full, dy_full = (
        lax.all_gather(x_feat, "mp", axis=0, tiled=True),
        lax.all_gather(grad_out, "mp", axis=0, tiled=True),
    )
    block_rows = x_full.shape[0] // BS
    x_blocks = x_full.reshape(block_rows, BS, row_count)
    dy_blocks = dy_full.reshape(block_rows, BS, row_count)
    gate_pre = spread_rows(w_gate, gate_blocks[:, 0], gate_blocks[:, 1], x_blocks, slot_cap)
    up_pre = spread_rows(w_up, up_blocks[:, 0], up_blocks[:, 1], x_blocks, slot_cap)
    sigma = jax.nn.sigmoid(gate_pre)
    gate_silu = gate_pre * sigma
    hidden = (gate_silu * up_pre).astype(jnp.bfloat16)
    up_prev = jnp.take(up_offsets, jnp.maximum(mp_index - 1, 0))
    up_low = jnp.take(up_offsets, mp_index)
    up_high = jnp.take(up_offsets, mp_index + 1)
    down_low = jnp.take(down_offsets, mp_index)
    down_high = jnp.take(down_offsets, mp_index + 1)
    slot_range = jnp.arange(slot_cap, dtype=jnp.int32)
    lower_hidden = shifted(hidden, "mp", 1)
    down_columns = down_low + slot_range
    hidden_down = pick_near(
        hidden,
        lower_hidden,
        up_low,
        up_prev,
        down_columns < up_low,
        down_columns,
        down_columns < down_high,
        slot_cap,
    )
    branch_part = (
        spread_rows(w_down, down_blocks[:, 1], down_blocks[:, 0], hidden_down, block_rows)
        * branch_scale
    )
    grad_hidden = (
        spread_back(w_down, down_blocks[:, 0], down_blocks[:, 1], dy_blocks, slot_cap)
        * branch_scale
    ).astype(jnp.bfloat16)
    down_piece = block_grads(
        hidden_down, down_blocks[:, 1], dy_blocks, down_blocks[:, 0], branch_scale * token_norm
    )
    upper_grad = shifted(grad_hidden, "mp", -1)
    up_columns = up_low + slot_range
    grad_local = pick_near(
        grad_hidden,
        upper_grad,
        down_low,
        down_high,
        up_columns >= down_high,
        up_columns,
        up_columns < up_high,
        slot_cap,
    )
    grad_hid_f = grad_local.astype(jnp.float32)
    grad_gate_pre = (grad_hid_f * up_pre * sigma * (1.0 + gate_pre * (1.0 - sigma))).astype(
        jnp.bfloat16
    )
    grad_up_pre = (grad_hid_f * gate_silu).astype(jnp.bfloat16)
    input_part = spread_back(
        w_gate, gate_blocks[:, 1], gate_blocks[:, 0], grad_gate_pre, block_rows
    )
    input_part = input_part + spread_back(
        w_up, up_blocks[:, 1], up_blocks[:, 0], grad_up_pre, block_rows
    )
    gate_piece = block_grads(
        x_blocks, gate_blocks[:, 0], grad_gate_pre, gate_blocks[:, 1], token_norm
    )
    up_piece = block_grads(x_blocks, up_blocks[:, 0], grad_up_pre, up_blocks[:, 1], token_norm)
    width_all = block_rows * BS
    branch_sum, input_sum = (
        lax.psum_scatter(
            branch_part.reshape(width_all, row_count).astype(jnp.bfloat16),
            "mp",
            scatter_dimension=0,
            tiled=True,
        ).astype(jnp.float32),
        lax.psum_scatter(
            input_part.reshape(width_all, row_count).astype(jnp.bfloat16),
            "mp",
            scatter_dimension=0,
            tiled=True,
        ).astype(jnp.float32),
    )
    down_total, gate_total, up_total = (
        reduce_pieces(down_piece, groups),
        reduce_pieces(gate_piece, groups),
        reduce_pieces(up_piece, groups),
    )
    return (
        branch_sum.astype(jnp.bfloat16),
        input_sum.astype(jnp.bfloat16),
        gate_total,
        up_total,
        down_total,
    )


def solution(mesh):
    in_specs = (
        P("mp", "dp"),
        P("mp", "dp"),
        P("mp", None),
        P("mp", None),
        P("mp", None),
        P("mp", None),
        P("mp", None),
        P("mp", None),
        P(),
        P(),
    )
    out_specs = (
        P("mp", "dp"),
        P("mp", "dp"),
        P(("mp", "dp"), None),
        P(("mp", "dp"), None),
        P(("mp", "dp"), None),
    )
    return jax.shard_map(local, mesh=mesh, in_specs=in_specs, out_specs=out_specs, check_vma=False)
```

```python
import math

import jax
import jax.numpy as jnp
from jax import lax
from jax.sharding import PartitionSpec as P

BS = 64
HC = 14


branch_scale = 1.0 / math.sqrt(80.0)


def shifted(value, axis, steps):
    count = lax.axis_size(axis)
    first, last = (max(0, -steps), min(count, count - steps))
    return lax.ppermute(value, axis, [(source, source + steps) for source in range(first, last)])


def segment_total(products, targets, out_count):
    choose = (targets[None, :] == jnp.arange(out_count, dtype=targets.dtype)[:, None]).astype(jnp.float32)
    return jnp.einsum(
        "sk,kor->sor",
        choose,
        products,
        precision=lax.Precision.HIGHEST,
        preferred_element_type=jnp.float32,
    )


def spread_rows(weights, pick_rows, targets, source, out_count):
    blocks = weights.reshape(weights.shape[0], BS, BS)
    pieces = jnp.take(source, pick_rows, axis=0)
    products = jnp.einsum("kir,kio->kor", pieces, blocks, preferred_element_type=jnp.float32)
    return segment_total(products, targets, out_count)


def spread_back(weights, pick_rows, targets, source, out_count):
    blocks = weights.reshape(weights.shape[0], BS, BS)
    pieces = jnp.take(source, pick_rows, axis=0)
    products = jnp.einsum("kor,kio->kir", pieces, blocks, preferred_element_type=jnp.float32)
    return segment_total(products, targets, out_count)


def block_grads(left_side, left_rows, right_side, right_rows, factor):
    first_pick = jnp.take(left_side, left_rows, axis=0)
    second_pick = jnp.take(right_side, right_rows, axis=0)
    products = jnp.einsum(
        "kir,kor->kio", first_pick, second_pick, preferred_element_type=jnp.float32
    )
    return (products * factor).astype(jnp.bfloat16).reshape(products.shape[0], BS * BS)


def split_groups(pieces, groups):
    return pieces.reshape(groups, pieces.shape[0] // groups, pieces.shape[1])


def reduce_pieces(pieces, groups):
    received = lax.all_to_all(
        split_groups(pieces, groups), "dp", split_axis=0, concat_axis=0, tiled=True
    )
    return jnp.sum(received, axis=0, dtype=jnp.float32)


def pick_near(own, other, own_low, other_low, use_other, columns, filled, slot_cap):
    stacked = jnp.concatenate([own, other], axis=0)
    position = jnp.where(use_other, slot_cap + columns - other_low, columns - own_low)
    position = jnp.clip(jnp.where(filled, position, 0), 0, 2 * slot_cap - 1)
    picked = jnp.take(stacked, position, axis=0)
    return jnp.where(filled[:, None, None], picked, jnp.zeros_like(picked))


def local(
    x_feat,
    grad_out,
    w_gate,
    w_up,
    w_down,
    gate_blocks,
    up_blocks,
    down_blocks,
    up_offsets,
    down_offsets,
):
    row_count = x_feat.shape[1]
    slot_cap = HC + 3
    groups = lax.axis_size("dp")
    mp_index = lax.axis_index("mp")
    token_norm = 1.0 / math.sqrt(row_count * groups)
    both = lax.all_gather(jnp.stack([x_feat, grad_out]), "mp", axis=0, tiled=False)
    x_full = both[:, 0].reshape(-1, row_count)
    dy_full = both[:, 1].reshape(-1, row_count)
    block_rows = x_full.shape[0] // BS
    x_blocks = x_full.reshape(block_rows, BS, row_count)
    dy_blocks = dy_full.reshape(block_rows, BS, row_count)
    gate_pre = spread_rows(w_gate, gate_blocks[:, 0], gate_blocks[:, 1], x_blocks, slot_cap)
    up_pre = spread_rows(w_up, up_blocks[:, 0], up_blocks[:, 1], x_blocks, slot_cap)
    sigma = jax.nn.sigmoid(gate_pre)
    gate_silu = gate_pre * sigma
    hidden = (gate_silu * up_pre).astype(jnp.bfloat16)
    up_prev = jnp.take(up_offsets, jnp.maximum(mp_index - 1, 0))
    up_low = jnp.take(up_offsets, mp_index)
    up_high = jnp.take(up_offsets, mp_index + 1)
    down_low = jnp.take(down_offsets, mp_index)
    down_high = jnp.take(down_offsets, mp_index + 1)
    slot_range = jnp.arange(slot_cap, dtype=jnp.int32)
    lower_hidden = shifted(hidden, "mp", 1)
    down_columns = down_low + slot_range
    hidden_down = pick_near(
        hidden,
        lower_hidden,
        up_low,
        up_prev,
        down_columns < up_low,
        down_columns,
        down_columns < down_high,
        slot_cap,
    )
    branch_part = (
        spread_rows(w_down, down_blocks[:, 1], down_blocks[:, 0], hidden_down, block_rows)
        * branch_scale
    )
    grad_hidden = (
        spread_back(w_down, down_blocks[:, 0], down_blocks[:, 1], dy_blocks, slot_cap)
        * branch_scale
    ).astype(jnp.bfloat16)
    down_piece = block_grads(
        hidden_down, down_blocks[:, 1], dy_blocks, down_blocks[:, 0], branch_scale * token_norm
    )
    upper_grad = shifted(grad_hidden, "mp", -1)
    up_columns = up_low + slot_range
    grad_local = pick_near(
        grad_hidden,
        upper_grad,
        down_low,
        down_high,
        up_columns >= down_high,
        up_columns,
        up_columns < up_high,
        slot_cap,
    )
    grad_hid_f = grad_local.astype(jnp.float32)
    grad_gate_pre = (grad_hid_f * up_pre * sigma * (1.0 + gate_pre * (1.0 - sigma))).astype(
        jnp.bfloat16
    )
    grad_up_pre = (grad_hid_f * gate_silu).astype(jnp.bfloat16)
    input_part = spread_back(
        w_gate, gate_blocks[:, 1], gate_blocks[:, 0], grad_gate_pre, block_rows
    )
    input_part = input_part + spread_back(
        w_up, up_blocks[:, 1], up_blocks[:, 0], grad_up_pre, block_rows
    )
    gate_piece = block_grads(
        x_blocks, gate_blocks[:, 0], grad_gate_pre, gate_blocks[:, 1], token_norm
    )
    up_piece = block_grads(x_blocks, up_blocks[:, 0], grad_up_pre, up_blocks[:, 1], token_norm)
    width_all = block_rows * BS
    branch_sum, input_sum = (
        lax.psum_scatter(
            branch_part.reshape(width_all, row_count).astype(jnp.bfloat16),
            "mp",
            scatter_dimension=0,
            tiled=True,
        ).astype(jnp.float32),
        lax.psum_scatter(
            input_part.reshape(width_all, row_count).astype(jnp.bfloat16),
            "mp",
            scatter_dimension=0,
            tiled=True,
        ).astype(jnp.float32),
    )
    down_total, gate_total, up_total = (
        reduce_pieces(down_piece, groups),
        reduce_pieces(gate_piece, groups),
        reduce_pieces(up_piece, groups),
    )
    return (
        branch_sum.astype(jnp.bfloat16),
        input_sum.astype(jnp.bfloat16),
        gate_total,
        up_total,
        down_total,
    )


def solution(mesh):
    in_specs = (
        P("mp", "dp"),
        P("mp", "dp"),
        P("mp", None),
        P("mp", None),
        P("mp", None),
        P("mp", None),
        P("mp", None),
        P("mp", None),
        P(),
        P(),
    )
    out_specs = (
        P("mp", "dp"),
        P("mp", "dp"),
        P(("mp", "dp"), None),
        P(("mp", "dp"), None),
        P(("mp", "dp"), None),
    )
    return jax.shard_map(local, mesh=mesh, in_specs=in_specs, out_specs=out_specs, check_vma=False)
```

```python
import math

import jax
import jax.numpy as jnp
from jax import lax
from jax.sharding import PartitionSpec as P

BS = 64
HC = 14


branch_scale = 1.0 / math.sqrt(80.0)


def shifted(value, axis, steps):
    count = lax.axis_size(axis)
    first, last = (max(0, -steps), min(count, count - steps))
    return lax.ppermute(value, axis, [(source, source + steps) for source in range(first, last)])


def segment_total(products, targets, out_count):
    choose = (targets[None, :] == jnp.arange(out_count, dtype=targets.dtype)[:, None]).astype(jnp.float32)
    return jnp.einsum(
        "sk,kor->sor",
        choose,
        products,
        precision=lax.Precision.HIGHEST,
        preferred_element_type=jnp.float32,
    )


def spread_rows(weights, pick_rows, targets, source, out_count):
    blocks = weights.reshape(weights.shape[0], BS, BS)
    pieces = jnp.take(source, pick_rows, axis=0)
    products = jnp.einsum("kir,kio->kor", pieces, blocks, preferred_element_type=jnp.float32)
    return segment_total(products, targets, out_count)


def spread_back(weights, pick_rows, targets, source, out_count):
    blocks = weights.reshape(weights.shape[0], BS, BS)
    pieces = jnp.take(source, pick_rows, axis=0)
    products = jnp.einsum("kor,kio->kir", pieces, blocks, preferred_element_type=jnp.float32)
    return segment_total(products, targets, out_count)


def block_grads(left_side, left_rows, right_side, right_rows, factor):
    first_pick = jnp.take(left_side, left_rows, axis=0)
    second_pick = jnp.take(right_side, right_rows, axis=0)
    products = jnp.einsum(
        "kir,kor->kio", first_pick, second_pick, preferred_element_type=jnp.float32
    )
    return (products * factor).astype(jnp.bfloat16).reshape(products.shape[0], BS * BS)


def split_groups(pieces, groups):
    return pieces.reshape(groups, pieces.shape[0] // groups, pieces.shape[1])


def reduce_pieces(pieces, groups):
    received = lax.all_to_all(
        split_groups(pieces, groups), "dp", split_axis=0, concat_axis=0, tiled=True
    )
    return jnp.sum(received, axis=0, dtype=jnp.float32)


def pick_near(own, other, own_low, other_low, use_other, columns, filled, slot_cap):
    stacked = jnp.concatenate([own, other], axis=0)
    position = jnp.where(use_other, slot_cap + columns - other_low, columns - own_low)
    position = jnp.clip(jnp.where(filled, position, 0), 0, 2 * slot_cap - 1)
    picked = jnp.take(stacked, position, axis=0)
    return jnp.where(filled[:, None, None], picked, jnp.zeros_like(picked))


def local(
    x_feat,
    grad_out,
    w_gate,
    w_up,
    w_down,
    gate_blocks,
    up_blocks,
    down_blocks,
    up_offsets,
    down_offsets,
):
    row_count = x_feat.shape[1]
    slot_cap = HC + 3
    groups = lax.axis_size("dp")
    mp_index = lax.axis_index("mp")
    token_norm = 1.0 / math.sqrt(row_count * groups)
    both = lax.all_gather(jnp.stack([x_feat, grad_out]), "mp", axis=0, tiled=False)
    x_full = both[:, 0].reshape(-1, row_count)
    dy_full = both[:, 1].reshape(-1, row_count)
    block_rows = x_full.shape[0] // BS
    x_blocks = x_full.reshape(block_rows, BS, row_count)
    dy_blocks = dy_full.reshape(block_rows, BS, row_count)
    gate_pre = spread_rows(w_gate, gate_blocks[:, 0], gate_blocks[:, 1], x_blocks, slot_cap)
    up_pre = spread_rows(w_up, up_blocks[:, 0], up_blocks[:, 1], x_blocks, slot_cap)
    sigma = jax.nn.sigmoid(gate_pre)
    gate_silu = gate_pre * sigma
    hidden = (gate_silu * up_pre).astype(jnp.bfloat16)
    up_prev = jnp.take(up_offsets, jnp.maximum(mp_index - 1, 0))
    up_low = jnp.take(up_offsets, mp_index)
    up_high = jnp.take(up_offsets, mp_index + 1)
    down_low = jnp.take(down_offsets, mp_index)
    down_high = jnp.take(down_offsets, mp_index + 1)
    slot_range = jnp.arange(slot_cap, dtype=jnp.int32)
    lower_hidden = shifted(hidden, "mp", 1)
    down_columns = down_low + slot_range
    hidden_down = pick_near(
        hidden,
        lower_hidden,
        up_low,
        up_prev,
        down_columns < up_low,
        down_columns,
        down_columns < down_high,
        slot_cap,
    )
    branch_part = (
        spread_rows(w_down, down_blocks[:, 1], down_blocks[:, 0], hidden_down, block_rows)
        * branch_scale
    )
    grad_hidden = (
        spread_back(w_down, down_blocks[:, 0], down_blocks[:, 1], dy_blocks, slot_cap)
        * branch_scale
    ).astype(jnp.bfloat16)
    down_piece = block_grads(
        hidden_down, down_blocks[:, 1], dy_blocks, down_blocks[:, 0], branch_scale * token_norm
    )
    upper_grad = shifted(grad_hidden, "mp", -1)
    up_columns = up_low + slot_range
    grad_local = pick_near(
        grad_hidden,
        upper_grad,
        down_low,
        down_high,
        up_columns >= down_high,
        up_columns,
        up_columns < up_high,
        slot_cap,
    )
    grad_hid_f = grad_local.astype(jnp.float32)
    grad_gate_pre = (grad_hid_f * up_pre * sigma * (1.0 + gate_pre * (1.0 - sigma))).astype(
        jnp.bfloat16
    )
    grad_up_pre = (grad_hid_f * gate_silu).astype(jnp.bfloat16)
    input_part = spread_back(
        w_gate, gate_blocks[:, 1], gate_blocks[:, 0], grad_gate_pre, block_rows
    )
    input_part = input_part + spread_back(
        w_up, up_blocks[:, 1], up_blocks[:, 0], grad_up_pre, block_rows
    )
    gate_piece = block_grads(
        x_blocks, gate_blocks[:, 0], grad_gate_pre, gate_blocks[:, 1], token_norm
    )
    up_piece = block_grads(x_blocks, up_blocks[:, 0], grad_up_pre, up_blocks[:, 1], token_norm)
    width_all = block_rows * BS
    branch_sum, input_sum = (
        lax.psum_scatter(
            branch_part.reshape(width_all, row_count).astype(jnp.bfloat16),
            "mp",
            scatter_dimension=0,
            tiled=True,
        ).astype(jnp.float32),
        lax.psum_scatter(
            input_part.reshape(width_all, row_count).astype(jnp.bfloat16),
            "mp",
            scatter_dimension=0,
            tiled=True,
        ).astype(jnp.float32),
    )
    down_total = reduce_pieces(down_piece, groups)
    paired = jnp.stack([gate_piece, up_piece]).reshape(2, groups, -1, gate_piece.shape[1])
    paired_received = lax.all_to_all(
        paired.transpose(1, 0, 2, 3), "dp", split_axis=0, concat_axis=0, tiled=True
    )
    paired_total = jnp.sum(paired_received, axis=0, dtype=jnp.float32)
    gate_total, up_total = paired_total[0], paired_total[1]
    return (
        branch_sum.astype(jnp.bfloat16),
        input_sum.astype(jnp.bfloat16),
        gate_total,
        up_total,
        down_total,
    )


def solution(mesh):
    in_specs = (
        P("mp", "dp"),
        P("mp", "dp"),
        P("mp", None),
        P("mp", None),
        P("mp", None),
        P("mp", None),
        P("mp", None),
        P("mp", None),
        P(),
        P(),
    )
    out_specs = (
        P("mp", "dp"),
        P("mp", "dp"),
        P(("mp", "dp"), None),
        P(("mp", "dp"), None),
        P(("mp", "dp"), None),
    )
    return jax.shard_map(local, mesh=mesh, in_specs=in_specs, out_specs=out_specs, check_vma=False)
```

```python
import math

import jax
import jax.numpy as jnp
from jax import lax
from jax.sharding import PartitionSpec as P

BS = 64
HC = 14


branch_scale = 1.0 / math.sqrt(80.0)


def shifted(value, axis, steps):
    count = lax.axis_size(axis)
    first, last = (max(0, -steps), min(count, count - steps))
    return lax.ppermute(value, axis, [(source, source + steps) for source in range(first, last)])


def segment_total(products, targets, out_count):
    choose = (targets[None, :] == jnp.arange(out_count, dtype=targets.dtype)[:, None]).astype(jnp.float32)
    return jnp.einsum(
        "sk,kor->sor",
        choose,
        products,
        precision=lax.Precision.HIGHEST,
        preferred_element_type=jnp.float32,
    )


def spread_rows(weights, pick_rows, targets, source, out_count):
    blocks = weights.reshape(weights.shape[0], BS, BS)
    pieces = jnp.take(source, pick_rows, axis=0)
    products = jnp.einsum("kir,kio->kor", pieces, blocks, preferred_element_type=jnp.float32)
    return segment_total(products, targets, out_count)


def spread_back(weights, pick_rows, targets, source, out_count):
    blocks = weights.reshape(weights.shape[0], BS, BS)
    pieces = jnp.take(source, pick_rows, axis=0)
    products = jnp.einsum("kor,kio->kir", pieces, blocks, preferred_element_type=jnp.float32)
    return segment_total(products, targets, out_count)


def block_grads(left_side, left_rows, right_side, right_rows, factor):
    first_pick = jnp.take(left_side, left_rows, axis=0)
    second_pick = jnp.take(right_side, right_rows, axis=0)
    products = jnp.einsum(
        "kir,kor->kio", first_pick, second_pick, preferred_element_type=jnp.float32
    )
    return (products * factor).astype(jnp.bfloat16).reshape(products.shape[0], BS * BS)


def split_groups(pieces, groups):
    return pieces.reshape(groups, pieces.shape[0] // groups, pieces.shape[1])


def reduce_pieces(pieces, groups):
    received = lax.all_to_all(
        split_groups(pieces, groups), "dp", split_axis=0, concat_axis=0, tiled=True
    )
    return jnp.sum(received, axis=0, dtype=jnp.float32)


def pick_near(own, other, own_low, other_low, use_other, columns, filled, slot_cap):
    stacked = jnp.concatenate([own, other], axis=0)
    position = jnp.where(use_other, slot_cap + columns - other_low, columns - own_low)
    position = jnp.clip(jnp.where(filled, position, 0), 0, 2 * slot_cap - 1)
    picked = jnp.take(stacked, position, axis=0)
    return jnp.where(filled[:, None, None], picked, jnp.zeros_like(picked))


def local(
    x_feat,
    grad_out,
    w_gate,
    w_up,
    w_down,
    gate_blocks,
    up_blocks,
    down_blocks,
    up_offsets,
    down_offsets,
):
    row_count = x_feat.shape[1]
    slot_cap = HC + 3
    groups = lax.axis_size("dp")
    mp_index = lax.axis_index("mp")
    token_norm = 1.0 / math.sqrt(row_count * groups)
    both = lax.all_gather(jnp.stack([x_feat, grad_out]), "mp", axis=0, tiled=False)
    x_full = both[:, 0].reshape(-1, row_count)
    dy_full = both[:, 1].reshape(-1, row_count)
    block_rows = x_full.shape[0] // BS
    x_blocks = x_full.reshape(block_rows, BS, row_count)
    dy_blocks = dy_full.reshape(block_rows, BS, row_count)
    gate_pre = spread_rows(w_gate, gate_blocks[:, 0], gate_blocks[:, 1], x_blocks, slot_cap)
    up_pre = spread_rows(w_up, up_blocks[:, 0], up_blocks[:, 1], x_blocks, slot_cap)
    sigma = jax.nn.sigmoid(gate_pre)
    gate_silu = gate_pre * sigma
    hidden = (gate_silu * up_pre).astype(jnp.bfloat16)
    up_prev = jnp.take(up_offsets, jnp.maximum(mp_index - 1, 0))
    up_low = jnp.take(up_offsets, mp_index)
    up_high = jnp.take(up_offsets, mp_index + 1)
    down_low = jnp.take(down_offsets, mp_index)
    down_high = jnp.take(down_offsets, mp_index + 1)
    slot_range = jnp.arange(slot_cap, dtype=jnp.int32)
    lower_hidden = shifted(hidden, "mp", 1)
    down_columns = down_low + slot_range
    hidden_down = pick_near(
        hidden,
        lower_hidden,
        up_low,
        up_prev,
        down_columns < up_low,
        down_columns,
        down_columns < down_high,
        slot_cap,
    )
    branch_part = (
        spread_rows(w_down, down_blocks[:, 1], down_blocks[:, 0], hidden_down, block_rows)
        * branch_scale
    )
    grad_hidden = (
        spread_back(w_down, down_blocks[:, 0], down_blocks[:, 1], dy_blocks, slot_cap)
        * branch_scale
    ).astype(jnp.bfloat16)
    down_piece = block_grads(
        hidden_down, down_blocks[:, 1], dy_blocks, down_blocks[:, 0], branch_scale * token_norm
    )
    upper_grad = shifted(grad_hidden, "mp", -1)
    up_columns = up_low + slot_range
    grad_local = pick_near(
        grad_hidden,
        upper_grad,
        down_low,
        down_high,
        up_columns >= down_high,
        up_columns,
        up_columns < up_high,
        slot_cap,
    )
    grad_hid_f = grad_local.astype(jnp.float32)
    grad_gate_pre = (grad_hid_f * up_pre * sigma * (1.0 + gate_pre * (1.0 - sigma))).astype(
        jnp.bfloat16
    )
    grad_up_pre = (grad_hid_f * gate_silu).astype(jnp.bfloat16)
    input_part = spread_back(
        w_gate, gate_blocks[:, 1], gate_blocks[:, 0], grad_gate_pre, block_rows
    )
    input_part = input_part + spread_back(
        w_up, up_blocks[:, 1], up_blocks[:, 0], grad_up_pre, block_rows
    )
    gate_piece = block_grads(
        x_blocks, gate_blocks[:, 0], grad_gate_pre, gate_blocks[:, 1], token_norm
    )
    up_piece = block_grads(x_blocks, up_blocks[:, 0], grad_up_pre, up_blocks[:, 1], token_norm)
    width_all = block_rows * BS
    mp_count = lax.axis_size("mp")
    both_parts = jnp.stack(
        [
            branch_part.reshape(mp_count, width_all // mp_count, row_count).astype(jnp.bfloat16),
            input_part.reshape(mp_count, width_all // mp_count, row_count).astype(jnp.bfloat16),
        ],
        axis=1,
    )
    both_sums = lax.psum_scatter(
        both_parts.reshape(2 * width_all, row_count), "mp", scatter_dimension=0, tiled=True
    ).reshape(2, width_all // mp_count, row_count)
    branch_sum = both_sums[0].astype(jnp.float32)
    input_sum = both_sums[1].astype(jnp.float32)
    down_total = reduce_pieces(down_piece, groups)
    paired = jnp.stack([gate_piece, up_piece]).reshape(2, groups, -1, gate_piece.shape[1])
    paired_received = lax.all_to_all(
        paired.transpose(1, 0, 2, 3), "dp", split_axis=0, concat_axis=0, tiled=True
    )
    paired_total = jnp.sum(paired_received, axis=0, dtype=jnp.float32)
    gate_total, up_total = paired_total[0], paired_total[1]
    return (
        branch_sum.astype(jnp.bfloat16),
        input_sum.astype(jnp.bfloat16),
        gate_total,
        up_total,
        down_total,
    )


def solution(mesh):
    in_specs = (
        P("mp", "dp"),
        P("mp", "dp"),
        P("mp", None),
        P("mp", None),
        P("mp", None),
        P("mp", None),
        P("mp", None),
        P("mp", None),
        P(),
        P(),
    )
    out_specs = (
        P("mp", "dp"),
        P("mp", "dp"),
        P(("mp", "dp"), None),
        P(("mp", "dp"), None),
        P(("mp", "dp"), None),
    )
    return jax.shard_map(local, mesh=mesh, in_specs=in_specs, out_specs=out_specs, check_vma=False)
```

```python
import math

import jax
import jax.numpy as jnp
from jax import lax
from jax.sharding import PartitionSpec as P

BS = 64
HC = 14


branch_scale = 1.0 / math.sqrt(80.0)


def shifted(value, axis, steps):
    count = lax.axis_size(axis)
    first, last = (max(0, -steps), min(count, count - steps))
    return lax.ppermute(value, axis, [(source, source + steps) for source in range(first, last)])


def segment_total(products, targets, out_count):
    choose = (targets[None, :] == jnp.arange(out_count, dtype=targets.dtype)[:, None]).astype(jnp.float32)
    return jnp.einsum(
        "sk,kor->sor",
        choose,
        products,
        precision=lax.Precision.HIGHEST,
        preferred_element_type=jnp.float32,
    )


def spread_rows(weights, pick_rows, targets, source, out_count):
    blocks = weights.reshape(weights.shape[0], BS, BS)
    pieces = jnp.take(source, pick_rows, axis=0)
    products = jnp.einsum("kir,kio->kor", pieces, blocks, preferred_element_type=jnp.float32)
    return segment_total(products, targets, out_count)


def spread_back(weights, pick_rows, targets, source, out_count):
    blocks = weights.reshape(weights.shape[0], BS, BS)
    pieces = jnp.take(source, pick_rows, axis=0)
    products = jnp.einsum("kor,kio->kir", pieces, blocks, preferred_element_type=jnp.float32)
    return segment_total(products, targets, out_count)


def block_grads(left_side, left_rows, right_side, right_rows, factor):
    first_pick = jnp.take(left_side, left_rows, axis=0)
    second_pick = jnp.take(right_side, right_rows, axis=0)
    products = jnp.einsum(
        "kir,kor->kio", first_pick, second_pick, preferred_element_type=jnp.float32
    )
    return (products * factor).astype(jnp.bfloat16).reshape(products.shape[0], BS * BS)


def split_groups(pieces, groups):
    return pieces.reshape(groups, pieces.shape[0] // groups, pieces.shape[1])


def reduce_pieces(pieces, groups):
    received = lax.all_to_all(
        split_groups(pieces, groups), "dp", split_axis=0, concat_axis=0, tiled=True
    )
    return jnp.sum(received, axis=0, dtype=jnp.float32)


def pick_near(own, other, own_low, other_low, use_other, columns, filled, slot_cap):
    stacked = jnp.concatenate([own, other], axis=0)
    position = jnp.where(use_other, slot_cap + columns - other_low, columns - own_low)
    position = jnp.clip(jnp.where(filled, position, 0), 0, 2 * slot_cap - 1)
    picked = jnp.take(stacked, position, axis=0)
    return jnp.where(filled[:, None, None], picked, jnp.zeros_like(picked))


def local(
    x_feat,
    grad_out,
    w_gate,
    w_up,
    w_down,
    gate_blocks,
    up_blocks,
    down_blocks,
    up_offsets,
    down_offsets,
):
    row_count = x_feat.shape[1]
    slot_cap = HC + 3
    groups = lax.axis_size("dp")
    mp_index = lax.axis_index("mp")
    token_norm = 1.0 / math.sqrt(row_count * groups)
    both = lax.all_gather(jnp.stack([x_feat, grad_out]), "mp", axis=0, tiled=False)
    x_full = both[:, 0].reshape(-1, row_count)
    dy_full = both[:, 1].reshape(-1, row_count)
    block_rows = x_full.shape[0] // BS
    x_blocks = x_full.reshape(block_rows, BS, row_count)
    dy_blocks = dy_full.reshape(block_rows, BS, row_count)
    gate_pre = spread_rows(w_gate, gate_blocks[:, 0], gate_blocks[:, 1], x_blocks, slot_cap)
    up_pre = spread_rows(w_up, up_blocks[:, 0], up_blocks[:, 1], x_blocks, slot_cap)
    sigma = jax.nn.sigmoid(gate_pre)
    gate_silu = gate_pre * sigma
    hidden = (gate_silu * up_pre).astype(jnp.bfloat16)
    up_prev = jnp.take(up_offsets, jnp.maximum(mp_index - 1, 0))
    up_low = jnp.take(up_offsets, mp_index)
    up_high = jnp.take(up_offsets, mp_index + 1)
    down_low = jnp.take(down_offsets, mp_index)
    down_high = jnp.take(down_offsets, mp_index + 1)
    slot_range = jnp.arange(slot_cap, dtype=jnp.int32)
    lower_hidden = shifted(hidden, "mp", 1)
    down_columns = down_low + slot_range
    hidden_down = pick_near(
        hidden,
        lower_hidden,
        up_low,
        up_prev,
        down_columns < up_low,
        down_columns,
        down_columns < down_high,
        slot_cap,
    )
    branch_part = (
        spread_rows(w_down, down_blocks[:, 1], down_blocks[:, 0], hidden_down, block_rows)
        * branch_scale
    )
    grad_hidden = (
        spread_back(w_down, down_blocks[:, 0], down_blocks[:, 1], dy_blocks, slot_cap)
        * branch_scale
    ).astype(jnp.bfloat16)
    down_piece = block_grads(
        hidden_down, down_blocks[:, 1], dy_blocks, down_blocks[:, 0], branch_scale * token_norm
    )
    upper_grad = shifted(grad_hidden, "mp", -1)
    up_columns = up_low + slot_range
    grad_local = pick_near(
        grad_hidden,
        upper_grad,
        down_low,
        down_high,
        up_columns >= down_high,
        up_columns,
        up_columns < up_high,
        slot_cap,
    )
    grad_hid_f = grad_local.astype(jnp.float32)
    grad_gate_pre = (grad_hid_f * up_pre * sigma * (1.0 + gate_pre * (1.0 - sigma))).astype(
        jnp.bfloat16
    )
    grad_up_pre = (grad_hid_f * gate_silu).astype(jnp.bfloat16)
    input_part = spread_back(
        w_gate, gate_blocks[:, 1], gate_blocks[:, 0], grad_gate_pre, block_rows
    )
    input_part = input_part + spread_back(
        w_up, up_blocks[:, 1], up_blocks[:, 0], grad_up_pre, block_rows
    )
    gate_piece = block_grads(
        x_blocks, gate_blocks[:, 0], grad_gate_pre, gate_blocks[:, 1], token_norm
    )
    up_piece = block_grads(x_blocks, up_blocks[:, 0], grad_up_pre, up_blocks[:, 1], token_norm)
    width_all = block_rows * BS
    mp_count = lax.axis_size("mp")
    both_parts = jnp.stack(
        [
            branch_part.reshape(mp_count, width_all // mp_count, row_count).astype(jnp.bfloat16),
            input_part.reshape(mp_count, width_all // mp_count, row_count).astype(jnp.bfloat16),
        ],
        axis=1,
    )
    both_sums = lax.psum_scatter(
        both_parts.reshape(2 * width_all, row_count), "mp", scatter_dimension=0, tiled=True
    ).reshape(2, width_all // mp_count, row_count)
    branch_sum = both_sums[0].astype(jnp.float32)
    input_sum = both_sums[1].astype(jnp.float32)
    grouped = jnp.stack([gate_piece, up_piece, down_piece]).reshape(
        3, groups, -1, gate_piece.shape[1]
    )
    grouped_received = lax.all_to_all(
        grouped.transpose(1, 0, 2, 3), "dp", split_axis=0, concat_axis=0, tiled=True
    )
    grouped_total = jnp.sum(grouped_received, axis=0, dtype=jnp.float32)
    gate_total, up_total, down_total = grouped_total[0], grouped_total[1], grouped_total[2]
    return (
        branch_sum.astype(jnp.bfloat16),
        input_sum.astype(jnp.bfloat16),
        gate_total,
        up_total,
        down_total,
    )


def solution(mesh):
    in_specs = (
        P("mp", "dp"),
        P("mp", "dp"),
        P("mp", None),
        P("mp", None),
        P("mp", None),
        P("mp", None),
        P("mp", None),
        P("mp", None),
        P(),
        P(),
    )
    out_specs = (
        P("mp", "dp"),
        P("mp", "dp"),
        P(("mp", "dp"), None),
        P(("mp", "dp"), None),
        P(("mp", "dp"), None),
    )
    return jax.shard_map(local, mesh=mesh, in_specs=in_specs, out_specs=out_specs, check_vma=False)
```

```python
import math

import jax
import jax.numpy as jnp
from jax import lax
from jax.sharding import PartitionSpec as P

BS = 64
HC = 14


branch_scale = 1.0 / math.sqrt(80.0)


def shifted(value, axis, steps):
    count = lax.axis_size(axis)
    first, last = (max(0, -steps), min(count, count - steps))
    return lax.ppermute(value, axis, [(source, source + steps) for source in range(first, last)])


def segment_total(products, targets, out_count):
    choose = (targets[None, :] == jnp.arange(out_count, dtype=targets.dtype)[:, None]).astype(jnp.float32)
    return jnp.einsum(
        "sk,kor->sor",
        choose,
        products,
        precision=lax.Precision.HIGHEST,
        preferred_element_type=jnp.float32,
    )


def spread_rows(weights, pick_rows, targets, source, out_count):
    blocks = weights.reshape(weights.shape[0], BS, BS)
    pieces = jnp.take(source, pick_rows, axis=0)
    products = jnp.einsum("kir,kio->kor", pieces, blocks, preferred_element_type=jnp.float32)
    return segment_total(products, targets, out_count)


def spread_back(weights, pick_rows, targets, source, out_count):
    blocks = weights.reshape(weights.shape[0], BS, BS)
    pieces = jnp.take(source, pick_rows, axis=0)
    products = jnp.einsum("kor,kio->kir", pieces, blocks, preferred_element_type=jnp.float32)
    return segment_total(products, targets, out_count)


def block_grads(left_side, left_rows, right_side, right_rows, factor):
    first_pick = jnp.take(left_side, left_rows, axis=0)
    second_pick = jnp.take(right_side, right_rows, axis=0)
    products = jnp.einsum(
        "kir,kor->kio", first_pick, second_pick, preferred_element_type=jnp.float32
    )
    return (products * factor).astype(jnp.bfloat16).reshape(products.shape[0], BS * BS)


def split_groups(pieces, groups):
    return pieces.reshape(groups, pieces.shape[0] // groups, pieces.shape[1])


def reduce_pieces(pieces, groups):
    received = lax.all_to_all(
        split_groups(pieces, groups), "dp", split_axis=0, concat_axis=0, tiled=True
    )
    return jnp.sum(received, axis=0, dtype=jnp.float32)


def pick_near(own, other, own_low, other_low, use_other, columns, filled, slot_cap):
    stacked = jnp.concatenate([own, other], axis=0)
    position = jnp.where(use_other, slot_cap + columns - other_low, columns - own_low)
    position = jnp.clip(jnp.where(filled, position, 0), 0, 2 * slot_cap - 1)
    picked = jnp.take(stacked, position, axis=0)
    return jnp.where(filled[:, None, None], picked, jnp.zeros_like(picked))


def local(
    x_feat,
    grad_out,
    w_gate,
    w_up,
    w_down,
    gate_blocks,
    up_blocks,
    down_blocks,
    up_offsets,
    down_offsets,
):
    row_count = x_feat.shape[1]
    slot_cap = HC + 3
    groups = lax.axis_size("dp")
    mp_index = lax.axis_index("mp")
    token_norm = 1.0 / math.sqrt(row_count * groups)
    both = lax.all_gather(jnp.stack([x_feat, grad_out]), "mp", axis=0, tiled=False)
    x_full = both[:, 0].reshape(-1, row_count)
    dy_full = both[:, 1].reshape(-1, row_count)
    block_rows = x_full.shape[0] // BS
    x_blocks = x_full.reshape(block_rows, BS, row_count)
    dy_blocks = dy_full.reshape(block_rows, BS, row_count)
    grad_hidden = (
        spread_back(w_down, down_blocks[:, 0], down_blocks[:, 1], dy_blocks, slot_cap)
        * branch_scale
    ).astype(jnp.bfloat16)
    grad_hidden, x_blocks = lax.optimization_barrier((grad_hidden, x_blocks))
    upper_grad = shifted(grad_hidden, "mp", -1)
    gate_pre = spread_rows(w_gate, gate_blocks[:, 0], gate_blocks[:, 1], x_blocks, slot_cap)
    up_pre = spread_rows(w_up, up_blocks[:, 0], up_blocks[:, 1], x_blocks, slot_cap)
    sigma = jax.nn.sigmoid(gate_pre)
    gate_silu = gate_pre * sigma
    hidden = (gate_silu * up_pre).astype(jnp.bfloat16)
    up_prev = jnp.take(up_offsets, jnp.maximum(mp_index - 1, 0))
    up_low = jnp.take(up_offsets, mp_index)
    up_high = jnp.take(up_offsets, mp_index + 1)
    down_low = jnp.take(down_offsets, mp_index)
    down_high = jnp.take(down_offsets, mp_index + 1)
    slot_range = jnp.arange(slot_cap, dtype=jnp.int32)
    lower_hidden = shifted(hidden, "mp", 1)
    down_columns = down_low + slot_range
    hidden_down = pick_near(
        hidden,
        lower_hidden,
        up_low,
        up_prev,
        down_columns < up_low,
        down_columns,
        down_columns < down_high,
        slot_cap,
    )
    down_piece = block_grads(
        hidden_down, down_blocks[:, 1], dy_blocks, down_blocks[:, 0], branch_scale * token_norm
    )
    down_piece, hidden_down = lax.optimization_barrier((down_piece, hidden_down))
    branch_part = (
        spread_rows(w_down, down_blocks[:, 1], down_blocks[:, 0], hidden_down, block_rows)
        * branch_scale
    )
    up_columns = up_low + slot_range
    grad_local = pick_near(
        grad_hidden,
        upper_grad,
        down_low,
        down_high,
        up_columns >= down_high,
        up_columns,
        up_columns < up_high,
        slot_cap,
    )
    grad_hid_f = grad_local.astype(jnp.float32)
    grad_gate_pre = (grad_hid_f * up_pre * sigma * (1.0 + gate_pre * (1.0 - sigma))).astype(
        jnp.bfloat16
    )
    grad_up_pre = (grad_hid_f * gate_silu).astype(jnp.bfloat16)
    input_part = spread_back(
        w_gate, gate_blocks[:, 1], gate_blocks[:, 0], grad_gate_pre, block_rows
    )
    input_part = input_part + spread_back(
        w_up, up_blocks[:, 1], up_blocks[:, 0], grad_up_pre, block_rows
    )
    input_part, branch_part, grad_gate_pre, grad_up_pre = lax.optimization_barrier(
        (input_part, branch_part, grad_gate_pre, grad_up_pre)
    )
    gate_piece = block_grads(
        x_blocks, gate_blocks[:, 0], grad_gate_pre, gate_blocks[:, 1], token_norm
    )
    up_piece = block_grads(x_blocks, up_blocks[:, 0], grad_up_pre, up_blocks[:, 1], token_norm)
    width_all = block_rows * BS
    mp_count = lax.axis_size("mp")
    both_parts = jnp.stack(
        [
            branch_part.reshape(mp_count, width_all // mp_count, row_count).astype(jnp.bfloat16),
            input_part.reshape(mp_count, width_all // mp_count, row_count).astype(jnp.bfloat16),
        ],
        axis=1,
    )
    both_sums = lax.psum_scatter(
        both_parts.reshape(2 * width_all, row_count), "mp", scatter_dimension=0, tiled=True
    ).reshape(2, width_all // mp_count, row_count)
    branch_sum = both_sums[0].astype(jnp.float32)
    input_sum = both_sums[1].astype(jnp.float32)
    down_total = reduce_pieces(down_piece, groups)
    paired = jnp.stack([gate_piece, up_piece]).reshape(2, groups, -1, gate_piece.shape[1])
    paired_received = lax.all_to_all(
        paired.transpose(1, 0, 2, 3), "dp", split_axis=0, concat_axis=0, tiled=True
    )
    paired_total = jnp.sum(paired_received, axis=0, dtype=jnp.float32)
    gate_total, up_total = paired_total[0], paired_total[1]
    return (
        branch_sum.astype(jnp.bfloat16),
        input_sum.astype(jnp.bfloat16),
        gate_total,
        up_total,
        down_total,
    )


def solution(mesh):
    in_specs = (
        P("mp", "dp"),
        P("mp", "dp"),
        P("mp", None),
        P("mp", None),
        P("mp", None),
        P("mp", None),
        P("mp", None),
        P("mp", None),
        P(),
        P(),
    )
    out_specs = (
        P("mp", "dp"),
        P("mp", "dp"),
        P(("mp", "dp"), None),
        P(("mp", "dp"), None),
        P(("mp", "dp"), None),
    )
    return jax.shard_map(local, mesh=mesh, in_specs=in_specs, out_specs=out_specs, check_vma=False)
```

```python
import math

import jax
import jax.numpy as jnp
from jax import lax
from jax.sharding import PartitionSpec as P

BS = 64
HC = 14


branch_scale = 1.0 / math.sqrt(80.0)


def shifted(value, axis, steps):
    count = lax.axis_size(axis)
    first, last = (max(0, -steps), min(count, count - steps))
    return lax.ppermute(value, axis, [(source, source + steps) for source in range(first, last)])


def segment_total(products, targets, out_count):
    choose = (targets[None, :] == jnp.arange(out_count, dtype=targets.dtype)[:, None]).astype(jnp.float32)
    return jnp.einsum(
        "sk,kor->sor",
        choose,
        products,
        precision=lax.Precision.HIGH,
        preferred_element_type=jnp.float32,
    )


def spread_rows(weights, pick_rows, targets, source, out_count):
    blocks = weights.reshape(weights.shape[0], BS, BS)
    pieces = jnp.take(source, pick_rows, axis=0)
    products = jnp.einsum("kir,kio->kor", pieces, blocks, preferred_element_type=jnp.float32)
    return segment_total(products, targets, out_count)


def spread_back(weights, pick_rows, targets, source, out_count):
    blocks = weights.reshape(weights.shape[0], BS, BS)
    pieces = jnp.take(source, pick_rows, axis=0)
    products = jnp.einsum("kor,kio->kir", pieces, blocks, preferred_element_type=jnp.float32)
    return segment_total(products, targets, out_count)


def block_grads(left_side, left_rows, right_side, right_rows, factor):
    first_pick = jnp.take(left_side, left_rows, axis=0)
    second_pick = jnp.take(right_side, right_rows, axis=0)
    products = jnp.einsum(
        "kir,kor->kio", first_pick, second_pick, preferred_element_type=jnp.float32
    )
    return (products * factor).astype(jnp.bfloat16).reshape(products.shape[0], BS * BS)


def split_groups(pieces, groups):
    return pieces.reshape(groups, pieces.shape[0] // groups, pieces.shape[1])


def reduce_pieces(pieces, groups):
    received = lax.all_to_all(
        split_groups(pieces, groups), "dp", split_axis=0, concat_axis=0, tiled=True
    )
    return jnp.sum(received, axis=0, dtype=jnp.float32)


def pick_near(own, other, own_low, other_low, use_other, columns, filled, slot_cap):
    stacked = jnp.concatenate([own, other], axis=0)
    position = jnp.where(use_other, slot_cap + columns - other_low, columns - own_low)
    position = jnp.clip(jnp.where(filled, position, 0), 0, 2 * slot_cap - 1)
    picked = jnp.take(stacked, position, axis=0)
    return jnp.where(filled[:, None, None], picked, jnp.zeros_like(picked))


def local(
    x_feat,
    grad_out,
    w_gate,
    w_up,
    w_down,
    gate_blocks,
    up_blocks,
    down_blocks,
    up_offsets,
    down_offsets,
):
    row_count = x_feat.shape[1]
    slot_cap = HC + 3
    groups = lax.axis_size("dp")
    mp_index = lax.axis_index("mp")
    token_norm = 1.0 / math.sqrt(row_count * groups)
    both = lax.all_gather(jnp.stack([x_feat, grad_out]), "mp", axis=0, tiled=False)
    x_full = both[:, 0].reshape(-1, row_count)
    dy_full = both[:, 1].reshape(-1, row_count)
    block_rows = x_full.shape[0] // BS
    x_blocks = x_full.reshape(block_rows, BS, row_count)
    dy_blocks = dy_full.reshape(block_rows, BS, row_count)
    gate_pre = spread_rows(w_gate, gate_blocks[:, 0], gate_blocks[:, 1], x_blocks, slot_cap)
    up_pre = spread_rows(w_up, up_blocks[:, 0], up_blocks[:, 1], x_blocks, slot_cap)
    sigma = jax.nn.sigmoid(gate_pre)
    gate_silu = gate_pre * sigma
    hidden = (gate_silu * up_pre).astype(jnp.bfloat16)
    up_prev = jnp.take(up_offsets, jnp.maximum(mp_index - 1, 0))
    up_low = jnp.take(up_offsets, mp_index)
    up_high = jnp.take(up_offsets, mp_index + 1)
    down_low = jnp.take(down_offsets, mp_index)
    down_high = jnp.take(down_offsets, mp_index + 1)
    slot_range = jnp.arange(slot_cap, dtype=jnp.int32)
    lower_hidden = shifted(hidden, "mp", 1)
    down_columns = down_low + slot_range
    hidden_down = pick_near(
        hidden,
        lower_hidden,
        up_low,
        up_prev,
        down_columns < up_low,
        down_columns,
        down_columns < down_high,
        slot_cap,
    )
    branch_part = (
        spread_rows(w_down, down_blocks[:, 1], down_blocks[:, 0], hidden_down, block_rows)
        * branch_scale
    )
    grad_hidden = (
        spread_back(w_down, down_blocks[:, 0], down_blocks[:, 1], dy_blocks, slot_cap)
        * branch_scale
    ).astype(jnp.bfloat16)
    down_piece = block_grads(
        hidden_down, down_blocks[:, 1], dy_blocks, down_blocks[:, 0], branch_scale * token_norm
    )
    upper_grad = shifted(grad_hidden, "mp", -1)
    up_columns = up_low + slot_range
    grad_local = pick_near(
        grad_hidden,
        upper_grad,
        down_low,
        down_high,
        up_columns >= down_high,
        up_columns,
        up_columns < up_high,
        slot_cap,
    )
    grad_hid_f = grad_local.astype(jnp.float32)
    grad_gate_pre = (grad_hid_f * up_pre * sigma * (1.0 + gate_pre * (1.0 - sigma))).astype(
        jnp.bfloat16
    )
    grad_up_pre = (grad_hid_f * gate_silu).astype(jnp.bfloat16)
    input_part = spread_back(
        w_gate, gate_blocks[:, 1], gate_blocks[:, 0], grad_gate_pre, block_rows
    )
    input_part = input_part + spread_back(
        w_up, up_blocks[:, 1], up_blocks[:, 0], grad_up_pre, block_rows
    )
    gate_piece = block_grads(
        x_blocks, gate_blocks[:, 0], grad_gate_pre, gate_blocks[:, 1], token_norm
    )
    up_piece = block_grads(x_blocks, up_blocks[:, 0], grad_up_pre, up_blocks[:, 1], token_norm)
    width_all = block_rows * BS
    mp_count = lax.axis_size("mp")
    both_parts = jnp.stack(
        [
            branch_part.reshape(mp_count, width_all // mp_count, row_count).astype(jnp.bfloat16),
            input_part.reshape(mp_count, width_all // mp_count, row_count).astype(jnp.bfloat16),
        ],
        axis=1,
    )
    both_sums = lax.psum_scatter(
        both_parts.reshape(2 * width_all, row_count), "mp", scatter_dimension=0, tiled=True
    ).reshape(2, width_all // mp_count, row_count)
    branch_sum = both_sums[0].astype(jnp.float32)
    input_sum = both_sums[1].astype(jnp.float32)
    down_total = reduce_pieces(down_piece, groups)
    paired = jnp.stack([gate_piece, up_piece]).reshape(2, groups, -1, gate_piece.shape[1])
    paired_received = lax.all_to_all(
        paired.transpose(1, 0, 2, 3), "dp", split_axis=0, concat_axis=0, tiled=True
    )
    paired_total = jnp.sum(paired_received, axis=0, dtype=jnp.float32)
    gate_total, up_total = paired_total[0], paired_total[1]
    return (
        branch_sum.astype(jnp.bfloat16),
        input_sum.astype(jnp.bfloat16),
        gate_total,
        up_total,
        down_total,
    )


def solution(mesh):
    in_specs = (
        P("mp", "dp"),
        P("mp", "dp"),
        P("mp", None),
        P("mp", None),
        P("mp", None),
        P("mp", None),
        P("mp", None),
        P("mp", None),
        P(),
        P(),
    )
    out_specs = (
        P("mp", "dp"),
        P("mp", "dp"),
        P(("mp", "dp"), None),
        P(("mp", "dp"), None),
        P(("mp", "dp"), None),
    )
    return jax.shard_map(local, mesh=mesh, in_specs=in_specs, out_specs=out_specs, check_vma=False)
```

```python
import math

import jax
import jax.numpy as jnp
from jax import lax
from jax.sharding import PartitionSpec as P

BS = 64
HC = 14


branch_scale = 1.0 / math.sqrt(80.0)


def shifted(value, axis, steps):
    count = lax.axis_size(axis)
    first, last = (max(0, -steps), min(count, count - steps))
    return lax.ppermute(value, axis, [(source, source + steps) for source in range(first, last)])


def segment_total(products, targets, out_count):
    choose = (targets[None, :] == jnp.arange(out_count, dtype=targets.dtype)[:, None]).astype(jnp.float32)
    return jnp.einsum(
        "sk,kor->sor",
        choose,
        products,
        precision=lax.Precision.HIGH,
        preferred_element_type=jnp.float32,
    )


def spread_rows(weights, pick_rows, targets, source, out_count):
    blocks = weights.reshape(weights.shape[0], BS, BS)
    pieces = jnp.take(source, pick_rows, axis=0)
    products = jnp.einsum("kir,kio->kor", pieces, blocks, preferred_element_type=jnp.float32)
    return segment_total(products, targets, out_count)


def spread_back(weights, pick_rows, targets, source, out_count):
    blocks = weights.reshape(weights.shape[0], BS, BS)
    pieces = jnp.take(source, pick_rows, axis=0)
    products = jnp.einsum("kor,kio->kir", pieces, blocks, preferred_element_type=jnp.float32)
    return segment_total(products, targets, out_count)


def block_grads(left_side, left_rows, right_side, right_rows, factor):
    first_pick = jnp.take(left_side, left_rows, axis=0)
    second_pick = jnp.take(right_side, right_rows, axis=0)
    products = jnp.einsum(
        "kir,kor->kio", first_pick, second_pick, preferred_element_type=jnp.float32
    )
    return (products * factor).astype(jnp.bfloat16).reshape(products.shape[0], BS * BS)


def split_groups(pieces, groups):
    return pieces.reshape(groups, pieces.shape[0] // groups, pieces.shape[1])


def reduce_pieces(pieces, groups):
    received = lax.all_to_all(
        split_groups(pieces, groups), "dp", split_axis=0, concat_axis=0, tiled=True
    )
    return jnp.sum(received, axis=0, dtype=jnp.float32)


def pick_near(own, other, own_low, other_low, use_other, columns, filled, slot_cap):
    stacked = jnp.concatenate([own, other], axis=0)
    position = jnp.where(use_other, slot_cap + columns - other_low, columns - own_low)
    position = jnp.clip(jnp.where(filled, position, 0), 0, 2 * slot_cap - 1)
    picked = jnp.take(stacked, position, axis=0)
    return jnp.where(filled[:, None, None], picked, jnp.zeros_like(picked))


def local(
    x_feat,
    grad_out,
    w_gate,
    w_up,
    w_down,
    gate_blocks,
    up_blocks,
    down_blocks,
    up_offsets,
    down_offsets,
):
    row_count = x_feat.shape[1]
    slot_cap = HC + 3
    groups = lax.axis_size("dp")
    mp_index = lax.axis_index("mp")
    token_norm = 1.0 / math.sqrt(row_count * groups)
    both = lax.all_gather(jnp.stack([x_feat, grad_out]), "mp", axis=0, tiled=False)
    x_full = both[:, 0].reshape(-1, row_count)
    dy_full = both[:, 1].reshape(-1, row_count)
    block_rows = x_full.shape[0] // BS
    x_blocks = x_full.reshape(block_rows, BS, row_count)
    dy_blocks = dy_full.reshape(block_rows, BS, row_count)
    gate_pre = spread_rows(w_gate, gate_blocks[:, 0], gate_blocks[:, 1], x_blocks, slot_cap)
    up_pre = spread_rows(w_up, up_blocks[:, 0], up_blocks[:, 1], x_blocks, slot_cap)
    sigma = jax.nn.sigmoid(gate_pre)
    gate_silu = gate_pre * sigma
    hidden = (gate_silu * up_pre).astype(jnp.bfloat16)
    up_prev = jnp.take(up_offsets, jnp.maximum(mp_index - 1, 0))
    up_low = jnp.take(up_offsets, mp_index)
    up_high = jnp.take(up_offsets, mp_index + 1)
    down_low = jnp.take(down_offsets, mp_index)
    down_high = jnp.take(down_offsets, mp_index + 1)
    slot_range = jnp.arange(slot_cap, dtype=jnp.int32)
    lower_hidden = shifted(hidden, "mp", 1)
    down_columns = down_low + slot_range
    hidden_down = pick_near(
        hidden,
        lower_hidden,
        up_low,
        up_prev,
        down_columns < up_low,
        down_columns,
        down_columns < down_high,
        slot_cap,
    )
    branch_part = (
        spread_rows(w_down, down_blocks[:, 1], down_blocks[:, 0], hidden_down, block_rows)
        * branch_scale
    )
    down_piece = block_grads(
        hidden_down, down_blocks[:, 1], dy_blocks, down_blocks[:, 0], branch_scale * token_norm
    )
    down_piece, dy_late = lax.optimization_barrier((down_piece, dy_blocks))
    grad_hidden = (
        spread_back(w_down, down_blocks[:, 0], down_blocks[:, 1], dy_late, slot_cap)
        * branch_scale
    ).astype(jnp.bfloat16)
    upper_grad = shifted(grad_hidden, "mp", -1)
    up_columns = up_low + slot_range
    grad_local = pick_near(
        grad_hidden,
        upper_grad,
        down_low,
        down_high,
        up_columns >= down_high,
        up_columns,
        up_columns < up_high,
        slot_cap,
    )
    grad_hid_f = grad_local.astype(jnp.float32)
    grad_gate_pre = (grad_hid_f * up_pre * sigma * (1.0 + gate_pre * (1.0 - sigma))).astype(
        jnp.bfloat16
    )
    grad_up_pre = (grad_hid_f * gate_silu).astype(jnp.bfloat16)
    input_part = spread_back(
        w_gate, gate_blocks[:, 1], gate_blocks[:, 0], grad_gate_pre, block_rows
    )
    input_part = input_part + spread_back(
        w_up, up_blocks[:, 1], up_blocks[:, 0], grad_up_pre, block_rows
    )
    gate_piece = block_grads(
        x_blocks, gate_blocks[:, 0], grad_gate_pre, gate_blocks[:, 1], token_norm
    )
    up_piece = block_grads(x_blocks, up_blocks[:, 0], grad_up_pre, up_blocks[:, 1], token_norm)
    width_all = block_rows * BS
    mp_count = lax.axis_size("mp")
    both_parts = jnp.stack(
        [
            branch_part.reshape(mp_count, width_all // mp_count, row_count).astype(jnp.bfloat16),
            input_part.reshape(mp_count, width_all // mp_count, row_count).astype(jnp.bfloat16),
        ],
        axis=1,
    )
    both_sums = lax.psum_scatter(
        both_parts.reshape(2 * width_all, row_count), "mp", scatter_dimension=0, tiled=True
    ).reshape(2, width_all // mp_count, row_count)
    branch_sum = both_sums[0].astype(jnp.float32)
    input_sum = both_sums[1].astype(jnp.float32)
    down_total = reduce_pieces(down_piece, groups)
    paired = jnp.stack([gate_piece, up_piece]).reshape(2, groups, -1, gate_piece.shape[1])
    paired_received = lax.all_to_all(
        paired.transpose(1, 0, 2, 3), "dp", split_axis=0, concat_axis=0, tiled=True
    )
    paired_total = jnp.sum(paired_received, axis=0, dtype=jnp.float32)
    gate_total, up_total = paired_total[0], paired_total[1]
    return (
        branch_sum.astype(jnp.bfloat16),
        input_sum.astype(jnp.bfloat16),
        gate_total,
        up_total,
        down_total,
    )


def solution(mesh):
    in_specs = (
        P("mp", "dp"),
        P("mp", "dp"),
        P("mp", None),
        P("mp", None),
        P("mp", None),
        P("mp", None),
        P("mp", None),
        P("mp", None),
        P(),
        P(),
    )
    out_specs = (
        P("mp", "dp"),
        P("mp", "dp"),
        P(("mp", "dp"), None),
        P(("mp", "dp"), None),
        P(("mp", "dp"), None),
    )
    return jax.shard_map(local, mesh=mesh, in_specs=in_specs, out_specs=out_specs, check_vma=False)
```

```python
import math

import jax
import jax.numpy as jnp
from jax import lax
from jax.sharding import PartitionSpec as P

BS = 64
HC = 14


branch_scale = 1.0 / math.sqrt(80.0)


def shifted(value, axis, steps):
    count = lax.axis_size(axis)
    first, last = (max(0, -steps), min(count, count - steps))
    return lax.ppermute(value, axis, [(source, source + steps) for source in range(first, last)])


def segment_total(products, targets, out_count):
    choose = (targets[None, :] == jnp.arange(out_count, dtype=targets.dtype)[:, None]).astype(jnp.float32)
    return jnp.einsum(
        "sk,kor->sor",
        choose,
        products,
        precision=lax.Precision.HIGH,
        preferred_element_type=jnp.float32,
    )


def spread_rows(weights, pick_rows, targets, source, out_count):
    blocks = weights.reshape(weights.shape[0], BS, BS)
    pieces = jnp.take(source, pick_rows, axis=0)
    products = jnp.einsum("kir,kio->kor", pieces, blocks, preferred_element_type=jnp.float32)
    return segment_total(products, targets, out_count)


def spread_back(weights, pick_rows, targets, source, out_count):
    blocks = weights.reshape(weights.shape[0], BS, BS)
    pieces = jnp.take(source, pick_rows, axis=0)
    products = jnp.einsum("kor,kio->kir", pieces, blocks, preferred_element_type=jnp.float32)
    return segment_total(products, targets, out_count)


def block_grads(left_side, left_rows, right_side, right_rows, factor):
    first_pick = jnp.take(left_side, left_rows, axis=0)
    second_pick = jnp.take(right_side, right_rows, axis=0)
    products = jnp.einsum(
        "kir,kor->kio", first_pick, second_pick, preferred_element_type=jnp.float32
    )
    return (products * factor).astype(jnp.bfloat16).reshape(products.shape[0], BS * BS)


def split_groups(pieces, groups):
    return pieces.reshape(groups, pieces.shape[0] // groups, pieces.shape[1])


def reduce_pieces(pieces, groups):
    received = lax.all_to_all(
        split_groups(pieces, groups), "dp", split_axis=0, concat_axis=0, tiled=True
    )
    return jnp.sum(received, axis=0, dtype=jnp.float32)


def pick_near(own, other, own_low, other_low, use_other, columns, filled, slot_cap):
    stacked = jnp.concatenate([own, other], axis=0)
    position = jnp.where(use_other, slot_cap + columns - other_low, columns - own_low)
    position = jnp.clip(jnp.where(filled, position, 0), 0, 2 * slot_cap - 1)
    picked = jnp.take(stacked, position, axis=0)
    return jnp.where(filled[:, None, None], picked, jnp.zeros_like(picked))


def local(
    x_feat,
    grad_out,
    w_gate,
    w_up,
    w_down,
    gate_blocks,
    up_blocks,
    down_blocks,
    up_offsets,
    down_offsets,
):
    row_count = x_feat.shape[1]
    slot_cap = HC + 3
    groups = lax.axis_size("dp")
    mp_index = lax.axis_index("mp")
    token_norm = 1.0 / math.sqrt(row_count * groups)
    both = lax.all_gather(jnp.stack([x_feat, grad_out]), "mp", axis=0, tiled=False)
    x_full = both[:, 0].reshape(-1, row_count)
    dy_full = both[:, 1].reshape(-1, row_count)
    block_rows = x_full.shape[0] // BS
    x_blocks = x_full.reshape(block_rows, BS, row_count)
    dy_blocks = dy_full.reshape(block_rows, BS, row_count)
    gate_pre = spread_rows(w_gate, gate_blocks[:, 0], gate_blocks[:, 1], x_blocks, slot_cap)
    up_pre = spread_rows(w_up, up_blocks[:, 0], up_blocks[:, 1], x_blocks, slot_cap)
    sigma = jax.nn.sigmoid(gate_pre)
    gate_silu = gate_pre * sigma
    hidden = (gate_silu * up_pre).astype(jnp.bfloat16)
    up_prev = jnp.take(up_offsets, jnp.maximum(mp_index - 1, 0))
    up_low = jnp.take(up_offsets, mp_index)
    up_high = jnp.take(up_offsets, mp_index + 1)
    down_low = jnp.take(down_offsets, mp_index)
    down_high = jnp.take(down_offsets, mp_index + 1)
    slot_range = jnp.arange(slot_cap, dtype=jnp.int32)
    lower_hidden = shifted(hidden, "mp", 1)
    down_columns = down_low + slot_range
    hidden_down = pick_near(
        hidden,
        lower_hidden,
        up_low,
        up_prev,
        down_columns < up_low,
        down_columns,
        down_columns < down_high,
        slot_cap,
    )
    down_piece = block_grads(
        hidden_down, down_blocks[:, 1], dy_blocks, down_blocks[:, 0], branch_scale * token_norm
    )
    down_piece, dy_late, hidden_down = lax.optimization_barrier((down_piece, dy_blocks, hidden_down))
    branch_part = (
        spread_rows(w_down, down_blocks[:, 1], down_blocks[:, 0], hidden_down, block_rows)
        * branch_scale
    )
    grad_hidden = (
        spread_back(w_down, down_blocks[:, 0], down_blocks[:, 1], dy_late, slot_cap)
        * branch_scale
    ).astype(jnp.bfloat16)
    upper_grad = shifted(grad_hidden, "mp", -1)
    up_columns = up_low + slot_range
    grad_local = pick_near(
        grad_hidden,
        upper_grad,
        down_low,
        down_high,
        up_columns >= down_high,
        up_columns,
        up_columns < up_high,
        slot_cap,
    )
    grad_hid_f = grad_local.astype(jnp.float32)
    grad_gate_pre = (grad_hid_f * up_pre * sigma * (1.0 + gate_pre * (1.0 - sigma))).astype(
        jnp.bfloat16
    )
    grad_up_pre = (grad_hid_f * gate_silu).astype(jnp.bfloat16)
    input_part = spread_back(
        w_gate, gate_blocks[:, 1], gate_blocks[:, 0], grad_gate_pre, block_rows
    )
    input_part = input_part + spread_back(
        w_up, up_blocks[:, 1], up_blocks[:, 0], grad_up_pre, block_rows
    )
    input_part, branch_part, grad_gate_pre, grad_up_pre = lax.optimization_barrier(
        (input_part, branch_part, grad_gate_pre, grad_up_pre)
    )
    gate_piece = block_grads(
        x_blocks, gate_blocks[:, 0], grad_gate_pre, gate_blocks[:, 1], token_norm
    )
    up_piece = block_grads(x_blocks, up_blocks[:, 0], grad_up_pre, up_blocks[:, 1], token_norm)
    width_all = block_rows * BS
    mp_count = lax.axis_size("mp")
    both_parts = jnp.stack(
        [
            branch_part.reshape(mp_count, width_all // mp_count, row_count).astype(jnp.bfloat16),
            input_part.reshape(mp_count, width_all // mp_count, row_count).astype(jnp.bfloat16),
        ],
        axis=1,
    )
    both_sums = lax.psum_scatter(
        both_parts.reshape(2 * width_all, row_count), "mp", scatter_dimension=0, tiled=True
    ).reshape(2, width_all // mp_count, row_count)
    branch_sum = both_sums[0].astype(jnp.float32)
    input_sum = both_sums[1].astype(jnp.float32)
    down_total = reduce_pieces(down_piece, groups)
    paired = jnp.stack([gate_piece, up_piece]).reshape(2, groups, -1, gate_piece.shape[1])
    paired_received = lax.all_to_all(
        paired.transpose(1, 0, 2, 3), "dp", split_axis=0, concat_axis=0, tiled=True
    )
    paired_total = jnp.sum(paired_received, axis=0, dtype=jnp.float32)
    gate_total, up_total = paired_total[0], paired_total[1]
    return (
        branch_sum.astype(jnp.bfloat16),
        input_sum.astype(jnp.bfloat16),
        gate_total,
        up_total,
        down_total,
    )


def solution(mesh):
    in_specs = (
        P("mp", "dp"),
        P("mp", "dp"),
        P("mp", None),
        P("mp", None),
        P("mp", None),
        P("mp", None),
        P("mp", None),
        P("mp", None),
        P(),
        P(),
    )
    out_specs = (
        P("mp", "dp"),
        P("mp", "dp"),
        P(("mp", "dp"), None),
        P(("mp", "dp"), None),
        P(("mp", "dp"), None),
    )
    return jax.shard_map(local, mesh=mesh, in_specs=in_specs, out_specs=out_specs, check_vma=False)
```

```python
import math

import jax
import jax.numpy as jnp
from jax import lax
from jax.sharding import PartitionSpec as P

BS = 64
HC = 14


branch_scale = 1.0 / math.sqrt(80.0)


def shifted(value, axis, steps):
    count = lax.axis_size(axis)
    first, last = (max(0, -steps), min(count, count - steps))
    return lax.ppermute(value, axis, [(source, source + steps) for source in range(first, last)])


def segment_total(products, targets, out_count):
    choose = (targets[None, :] == jnp.arange(out_count, dtype=targets.dtype)[:, None]).astype(jnp.float32)
    return jnp.einsum(
        "sk,kor->sor",
        choose,
        products,
        precision=lax.Precision.HIGH,
        preferred_element_type=jnp.float32,
    )


def spread_rows(weights, pick_rows, targets, source, out_count):
    blocks = weights.reshape(weights.shape[0], BS, BS)
    pieces = jnp.take(source, pick_rows, axis=0)
    products = jnp.einsum("kir,kio->kor", pieces, blocks, preferred_element_type=jnp.float32)
    return segment_total(products, targets, out_count)


def spread_back(weights, pick_rows, targets, source, out_count):
    blocks = weights.reshape(weights.shape[0], BS, BS)
    pieces = jnp.take(source, pick_rows, axis=0)
    products = jnp.einsum("kor,kio->kir", pieces, blocks, preferred_element_type=jnp.float32)
    return segment_total(products, targets, out_count)


def block_grads(left_side, left_rows, right_side, right_rows, factor):
    first_pick = jnp.take(left_side, left_rows, axis=0)
    second_pick = jnp.take(right_side, right_rows, axis=0)
    products = jnp.einsum(
        "kir,kor->kio", first_pick, second_pick, preferred_element_type=jnp.float32
    )
    return (products * factor).astype(jnp.bfloat16).reshape(products.shape[0], BS * BS)


def split_groups(pieces, groups):
    return pieces.reshape(groups, pieces.shape[0] // groups, pieces.shape[1])


def reduce_pieces(pieces, groups):
    received = lax.all_to_all(
        split_groups(pieces, groups), "dp", split_axis=0, concat_axis=0, tiled=True
    )
    return jnp.sum(received, axis=0, dtype=jnp.float32)


def pick_near(own, other, own_low, other_low, use_other, columns, filled, slot_cap):
    stacked = jnp.concatenate([own, other], axis=0)
    position = jnp.where(use_other, slot_cap + columns - other_low, columns - own_low)
    position = jnp.clip(jnp.where(filled, position, 0), 0, 2 * slot_cap - 1)
    picked = jnp.take(stacked, position, axis=0)
    return jnp.where(filled[:, None, None], picked, jnp.zeros_like(picked))


def local(
    x_feat,
    grad_out,
    w_gate,
    w_up,
    w_down,
    gate_blocks,
    up_blocks,
    down_blocks,
    up_offsets,
    down_offsets,
):
    row_count = x_feat.shape[1]
    slot_cap = HC + 3
    groups = lax.axis_size("dp")
    mp_index = lax.axis_index("mp")
    token_norm = 1.0 / math.sqrt(row_count * groups)
    both = lax.all_gather(jnp.stack([x_feat, grad_out]), "mp", axis=0, tiled=False)
    x_full = both[:, 0].reshape(-1, row_count)
    dy_full = both[:, 1].reshape(-1, row_count)
    block_rows = x_full.shape[0] // BS
    x_blocks = x_full.reshape(block_rows, BS, row_count)
    dy_blocks = dy_full.reshape(block_rows, BS, row_count)
    gate_pre = spread_rows(w_gate, gate_blocks[:, 0], gate_blocks[:, 1], x_blocks, slot_cap)
    up_pre = spread_rows(w_up, up_blocks[:, 0], up_blocks[:, 1], x_blocks, slot_cap)
    sigma = jax.nn.sigmoid(gate_pre)
    gate_silu = gate_pre * sigma
    hidden = (gate_silu * up_pre).astype(jnp.bfloat16)
    up_prev = jnp.take(up_offsets, jnp.maximum(mp_index - 1, 0))
    up_low = jnp.take(up_offsets, mp_index)
    up_high = jnp.take(up_offsets, mp_index + 1)
    down_low = jnp.take(down_offsets, mp_index)
    down_high = jnp.take(down_offsets, mp_index + 1)
    slot_range = jnp.arange(slot_cap, dtype=jnp.int32)
    lower_hidden = shifted(hidden, "mp", 1)
    down_columns = down_low + slot_range
    hidden_down = pick_near(
        hidden,
        lower_hidden,
        up_low,
        up_prev,
        down_columns < up_low,
        down_columns,
        down_columns < down_high,
        slot_cap,
    )
    branch_part = (
        spread_rows(w_down, down_blocks[:, 1], down_blocks[:, 0], hidden_down, block_rows)
        * branch_scale
    )
    down_piece = block_grads(
        hidden_down, down_blocks[:, 1], dy_blocks, down_blocks[:, 0], branch_scale * token_norm
    )
    down_groups, dy_late = lax.optimization_barrier((split_groups(down_piece, groups), dy_blocks))
    grad_hidden = (
        spread_back(w_down, down_blocks[:, 0], down_blocks[:, 1], dy_late, slot_cap)
        * branch_scale
    ).astype(jnp.bfloat16)
    upper_grad = shifted(grad_hidden, "mp", -1)
    up_columns = up_low + slot_range
    grad_local = pick_near(
        grad_hidden,
        upper_grad,
        down_low,
        down_high,
        up_columns >= down_high,
        up_columns,
        up_columns < up_high,
        slot_cap,
    )
    grad_hid_f = grad_local.astype(jnp.float32)
    grad_gate_pre = (grad_hid_f * up_pre * sigma * (1.0 + gate_pre * (1.0 - sigma))).astype(
        jnp.bfloat16
    )
    grad_up_pre = (grad_hid_f * gate_silu).astype(jnp.bfloat16)
    input_part = spread_back(
        w_gate, gate_blocks[:, 1], gate_blocks[:, 0], grad_gate_pre, block_rows
    )
    input_part = input_part + spread_back(
        w_up, up_blocks[:, 1], up_blocks[:, 0], grad_up_pre, block_rows
    )
    gate_piece = block_grads(
        x_blocks, gate_blocks[:, 0], grad_gate_pre, gate_blocks[:, 1], token_norm
    )
    up_piece = block_grads(x_blocks, up_blocks[:, 0], grad_up_pre, up_blocks[:, 1], token_norm)
    width_all = block_rows * BS
    mp_count = lax.axis_size("mp")
    both_parts = jnp.stack(
        [
            branch_part.reshape(mp_count, width_all // mp_count, row_count).astype(jnp.bfloat16),
            input_part.reshape(mp_count, width_all // mp_count, row_count).astype(jnp.bfloat16),
        ],
        axis=1,
    )
    both_sums = lax.psum_scatter(
        both_parts.reshape(2 * width_all, row_count), "mp", scatter_dimension=0, tiled=True
    ).reshape(2, width_all // mp_count, row_count)
    branch_sum = both_sums[0].astype(jnp.float32)
    input_sum = both_sums[1].astype(jnp.float32)
    down_received = lax.all_to_all(down_groups, "dp", split_axis=0, concat_axis=0, tiled=True)
    down_total = jnp.sum(down_received, axis=0, dtype=jnp.float32)
    paired = jnp.stack([gate_piece, up_piece]).reshape(2, groups, -1, gate_piece.shape[1])
    paired_received = lax.all_to_all(
        paired.transpose(1, 0, 2, 3), "dp", split_axis=0, concat_axis=0, tiled=True
    )
    paired_total = jnp.sum(paired_received, axis=0, dtype=jnp.float32)
    gate_total, up_total = paired_total[0], paired_total[1]
    return (
        branch_sum.astype(jnp.bfloat16),
        input_sum.astype(jnp.bfloat16),
        gate_total,
        up_total,
        down_total,
    )


def solution(mesh):
    in_specs = (
        P("mp", "dp"),
        P("mp", "dp"),
        P("mp", None),
        P("mp", None),
        P("mp", None),
        P("mp", None),
        P("mp", None),
        P("mp", None),
        P(),
        P(),
    )
    out_specs = (
        P("mp", "dp"),
        P("mp", "dp"),
        P(("mp", "dp"), None),
        P(("mp", "dp"), None),
        P(("mp", "dp"), None),
    )
    return jax.shard_map(local, mesh=mesh, in_specs=in_specs, out_specs=out_specs, check_vma=False)
```

```python
import math

import jax
import jax.numpy as jnp
from jax import lax
from jax.sharding import PartitionSpec as P

BS = 64
HC = 14


branch_scale = 1.0 / math.sqrt(80.0)


def shifted(value, axis, steps):
    count = lax.axis_size(axis)
    first, last = (max(0, -steps), min(count, count - steps))
    return lax.ppermute(value, axis, [(source, source + steps) for source in range(first, last)])


def segment_total(products, targets, out_count):
    choose = (targets[None, :] == jnp.arange(out_count, dtype=targets.dtype)[:, None]).astype(jnp.float32)
    return jnp.einsum(
        "sk,kor->sor",
        choose,
        products,
        precision=lax.Precision.HIGH,
        preferred_element_type=jnp.float32,
    )


def spread_rows(weights, pick_rows, targets, source, out_count):
    blocks = weights.reshape(weights.shape[0], BS, BS)
    pieces = jnp.take(source, pick_rows, axis=0)
    products = jnp.einsum("kir,kio->kor", pieces, blocks, preferred_element_type=jnp.float32)
    return segment_total(products, targets, out_count)


def spread_back(weights, pick_rows, targets, source, out_count):
    blocks = weights.reshape(weights.shape[0], BS, BS)
    pieces = jnp.take(source, pick_rows, axis=0)
    products = jnp.einsum("kor,kio->kir", pieces, blocks, preferred_element_type=jnp.float32)
    return segment_total(products, targets, out_count)


def block_grads(left_side, left_rows, right_side, right_rows, factor):
    first_pick = jnp.take(left_side, left_rows, axis=0)
    second_pick = jnp.take(right_side, right_rows, axis=0)
    products = jnp.einsum(
        "kir,kor->kio", first_pick, second_pick, preferred_element_type=jnp.float32
    )
    return (products * factor).astype(jnp.bfloat16).reshape(products.shape[0], BS * BS)


def split_groups(pieces, groups):
    return pieces.reshape(groups, pieces.shape[0] // groups, pieces.shape[1])


def reduce_pieces(pieces, groups):
    received = lax.all_to_all(
        split_groups(pieces, groups), "dp", split_axis=0, concat_axis=0, tiled=True
    )
    return jnp.sum(received, axis=0, dtype=jnp.float32)


def pick_near(own, other, own_low, other_low, use_other, columns, filled, slot_cap):
    stacked = jnp.concatenate([own, other], axis=0)
    position = jnp.where(use_other, slot_cap + columns - other_low, columns - own_low)
    position = jnp.clip(jnp.where(filled, position, 0), 0, 2 * slot_cap - 1)
    picked = jnp.take(stacked, position, axis=0)
    return jnp.where(filled[:, None, None], picked, jnp.zeros_like(picked))


def local(
    x_feat,
    grad_out,
    w_gate,
    w_up,
    w_down,
    gate_blocks,
    up_blocks,
    down_blocks,
    up_offsets,
    down_offsets,
):
    row_count = x_feat.shape[1]
    slot_cap = HC + 3
    groups = lax.axis_size("dp")
    mp_index = lax.axis_index("mp")
    token_norm = 1.0 / math.sqrt(row_count * groups)
    both = lax.all_gather(jnp.stack([x_feat, grad_out]), "mp", axis=0, tiled=False)
    w_gate, w_up, w_down, both = lax.optimization_barrier(
        (w_gate.reshape(-1, BS, BS), w_up.reshape(-1, BS, BS), w_down.reshape(-1, BS, BS), both)
    )
    x_full = both[:, 0].reshape(-1, row_count)
    dy_full = both[:, 1].reshape(-1, row_count)
    block_rows = x_full.shape[0] // BS
    x_blocks = x_full.reshape(block_rows, BS, row_count)
    dy_blocks = dy_full.reshape(block_rows, BS, row_count)
    gate_pre = spread_rows(w_gate, gate_blocks[:, 0], gate_blocks[:, 1], x_blocks, slot_cap)
    up_pre = spread_rows(w_up, up_blocks[:, 0], up_blocks[:, 1], x_blocks, slot_cap)
    sigma = jax.nn.sigmoid(gate_pre)
    gate_silu = gate_pre * sigma
    hidden = (gate_silu * up_pre).astype(jnp.bfloat16)
    up_prev = jnp.take(up_offsets, jnp.maximum(mp_index - 1, 0))
    up_low = jnp.take(up_offsets, mp_index)
    up_high = jnp.take(up_offsets, mp_index + 1)
    down_low = jnp.take(down_offsets, mp_index)
    down_high = jnp.take(down_offsets, mp_index + 1)
    slot_range = jnp.arange(slot_cap, dtype=jnp.int32)
    lower_hidden = shifted(hidden, "mp", 1)
    down_columns = down_low + slot_range
    hidden_down = pick_near(
        hidden,
        lower_hidden,
        up_low,
        up_prev,
        down_columns < up_low,
        down_columns,
        down_columns < down_high,
        slot_cap,
    )
    branch_part = (
        spread_rows(w_down, down_blocks[:, 1], down_blocks[:, 0], hidden_down, block_rows)
        * branch_scale
    )
    down_piece = block_grads(
        hidden_down, down_blocks[:, 1], dy_blocks, down_blocks[:, 0], branch_scale * token_norm
    )
    down_groups, dy_late = lax.optimization_barrier((split_groups(down_piece, groups), dy_blocks))
    grad_hidden = (
        spread_back(w_down, down_blocks[:, 0], down_blocks[:, 1], dy_late, slot_cap)
        * branch_scale
    ).astype(jnp.bfloat16)
    upper_grad = shifted(grad_hidden, "mp", -1)
    up_columns = up_low + slot_range
    grad_local = pick_near(
        grad_hidden,
        upper_grad,
        down_low,
        down_high,
        up_columns >= down_high,
        up_columns,
        up_columns < up_high,
        slot_cap,
    )
    grad_hid_f = grad_local.astype(jnp.float32)
    grad_gate_pre = (grad_hid_f * up_pre * sigma * (1.0 + gate_pre * (1.0 - sigma))).astype(
        jnp.bfloat16
    )
    grad_up_pre = (grad_hid_f * gate_silu).astype(jnp.bfloat16)
    input_part = spread_back(
        w_gate, gate_blocks[:, 1], gate_blocks[:, 0], grad_gate_pre, block_rows
    )
    input_part = input_part + spread_back(
        w_up, up_blocks[:, 1], up_blocks[:, 0], grad_up_pre, block_rows
    )
    gate_piece = block_grads(
        x_blocks, gate_blocks[:, 0], grad_gate_pre, gate_blocks[:, 1], token_norm
    )
    up_piece = block_grads(x_blocks, up_blocks[:, 0], grad_up_pre, up_blocks[:, 1], token_norm)
    width_all = block_rows * BS
    mp_count = lax.axis_size("mp")
    both_parts = jnp.stack(
        [
            branch_part.reshape(mp_count, width_all // mp_count, row_count).astype(jnp.bfloat16),
            input_part.reshape(mp_count, width_all // mp_count, row_count).astype(jnp.bfloat16),
        ],
        axis=1,
    )
    both_sums = lax.psum_scatter(
        both_parts.reshape(2 * width_all, row_count), "mp", scatter_dimension=0, tiled=True
    ).reshape(2, width_all // mp_count, row_count)
    branch_sum = both_sums[0].astype(jnp.float32)
    input_sum = both_sums[1].astype(jnp.float32)
    down_received = lax.all_to_all(down_groups, "dp", split_axis=0, concat_axis=0, tiled=True)
    down_total = jnp.sum(down_received, axis=0, dtype=jnp.float32)
    paired = jnp.stack([gate_piece, up_piece]).reshape(2, groups, -1, gate_piece.shape[1])
    paired_received = lax.all_to_all(
        paired.transpose(1, 0, 2, 3), "dp", split_axis=0, concat_axis=0, tiled=True
    )
    paired_total = jnp.sum(paired_received, axis=0, dtype=jnp.float32)
    gate_total, up_total = paired_total[0], paired_total[1]
    return (
        branch_sum.astype(jnp.bfloat16),
        input_sum.astype(jnp.bfloat16),
        gate_total,
        up_total,
        down_total,
    )


def solution(mesh):
    in_specs = (
        P("mp", "dp"),
        P("mp", "dp"),
        P("mp", None),
        P("mp", None),
        P("mp", None),
        P("mp", None),
        P("mp", None),
        P("mp", None),
        P(),
        P(),
    )
    out_specs = (
        P("mp", "dp"),
        P("mp", "dp"),
        P(("mp", "dp"), None),
        P(("mp", "dp"), None),
        P(("mp", "dp"), None),
    )
    return jax.shard_map(local, mesh=mesh, in_specs=in_specs, out_specs=out_specs, check_vma=False)
```

```python
import math

import jax
import jax.numpy as jnp
from jax import lax
from jax.sharding import PartitionSpec as P

BS = 64
HC = 14


branch_scale = 1.0 / math.sqrt(80.0)


def shifted(value, axis, steps):
    count = lax.axis_size(axis)
    first, last = (max(0, -steps), min(count, count - steps))
    return lax.ppermute(value, axis, [(source, source + steps) for source in range(first, last)])


def segment_total(products, targets, out_count):
    choose = (targets[None, :] == jnp.arange(out_count, dtype=targets.dtype)[:, None]).astype(jnp.float32)
    return jnp.einsum(
        "sk,kor->sor",
        choose,
        products,
        precision=lax.Precision.HIGH,
        preferred_element_type=jnp.float32,
    )


def spread_rows(weights, pick_rows, targets, source, out_count):
    blocks = weights.reshape(weights.shape[0], BS, BS)
    pieces = jnp.take(source, pick_rows, axis=0)
    products = jnp.einsum("kir,kio->kor", pieces, blocks, preferred_element_type=jnp.float32)
    return segment_total(products, targets, out_count)


def spread_back(weights, pick_rows, targets, source, out_count):
    blocks = weights.reshape(weights.shape[0], BS, BS)
    pieces = jnp.take(source, pick_rows, axis=0)
    products = jnp.einsum("kor,kio->kir", pieces, blocks, preferred_element_type=jnp.float32)
    return segment_total(products, targets, out_count)


def block_grads(left_side, left_rows, right_side, right_rows, factor):
    first_pick = jnp.take(left_side, left_rows, axis=0)
    second_pick = jnp.take(right_side, right_rows, axis=0)
    products = jnp.einsum(
        "kir,kor->kio", first_pick, second_pick, preferred_element_type=jnp.float32
    )
    return (products * factor).astype(jnp.bfloat16).reshape(products.shape[0], BS * BS)


def split_groups(pieces, groups):
    return pieces.reshape(groups, pieces.shape[0] // groups, pieces.shape[1])


def reduce_pieces(pieces, groups):
    received = lax.all_to_all(
        split_groups(pieces, groups), "dp", split_axis=0, concat_axis=0, tiled=True
    )
    return jnp.sum(received, axis=0, dtype=jnp.float32)


def pick_near(own, other, own_low, other_low, use_other, columns, filled, slot_cap):
    stacked = jnp.concatenate([own, other], axis=0)
    position = jnp.where(use_other, slot_cap + columns - other_low, columns - own_low)
    position = jnp.clip(jnp.where(filled, position, 0), 0, 2 * slot_cap - 1)
    picked = jnp.take(stacked, position, axis=0)
    return jnp.where(filled[:, None, None], picked, jnp.zeros_like(picked))


def local(
    x_feat,
    grad_out,
    w_gate,
    w_up,
    w_down,
    gate_blocks,
    up_blocks,
    down_blocks,
    up_offsets,
    down_offsets,
):
    row_count = x_feat.shape[1]
    slot_cap = HC + 3
    groups = lax.axis_size("dp")
    mp_index = lax.axis_index("mp")
    token_norm = 1.0 / math.sqrt(row_count * groups)
    both = lax.all_gather(jnp.stack([x_feat, grad_out]), "mp", axis=0, tiled=False)
    w_gate, w_up, w_down, both = lax.optimization_barrier(
        (w_gate.reshape(-1, BS, BS), w_up.reshape(-1, BS, BS), w_down.reshape(-1, BS, BS), both)
    )
    x_full = both[:, 0].reshape(-1, row_count)
    dy_full = both[:, 1].reshape(-1, row_count)
    block_rows = x_full.shape[0] // BS
    x_blocks = x_full.reshape(block_rows, BS, row_count)
    dy_blocks = dy_full.reshape(block_rows, BS, row_count)
    gate_pre = spread_rows(w_gate, gate_blocks[:, 0], gate_blocks[:, 1], x_blocks, slot_cap)
    up_pre = spread_rows(w_up, up_blocks[:, 0], up_blocks[:, 1], x_blocks, slot_cap)
    sigma = jax.nn.sigmoid(gate_pre)
    gate_silu = gate_pre * sigma
    hidden = (gate_silu * up_pre).astype(jnp.bfloat16)
    up_prev = jnp.take(up_offsets, jnp.maximum(mp_index - 1, 0))
    up_low = jnp.take(up_offsets, mp_index)
    up_high = jnp.take(up_offsets, mp_index + 1)
    down_low = jnp.take(down_offsets, mp_index)
    down_high = jnp.take(down_offsets, mp_index + 1)
    slot_range = jnp.arange(slot_cap, dtype=jnp.int32)
    lower_hidden = shifted(hidden, "mp", 1)
    down_columns = down_low + slot_range
    hidden_down = pick_near(
        hidden,
        lower_hidden,
        up_low,
        up_prev,
        down_columns < up_low,
        down_columns,
        down_columns < down_high,
        slot_cap,
    )
    branch_part = (
        spread_rows(w_down, down_blocks[:, 1], down_blocks[:, 0], hidden_down, block_rows)
        * branch_scale
    )
    down_piece = block_grads(
        hidden_down, down_blocks[:, 1], dy_blocks, down_blocks[:, 0], branch_scale * token_norm
    )
    down_groups, dy_late = lax.optimization_barrier((split_groups(down_piece, groups), dy_blocks))
    grad_hidden = (
        spread_back(w_down, down_blocks[:, 0], down_blocks[:, 1], dy_late, slot_cap)
        * branch_scale
    ).astype(jnp.bfloat16)
    upper_grad = shifted(grad_hidden, "mp", -1)
    up_columns = up_low + slot_range
    grad_local = pick_near(
        grad_hidden,
        upper_grad,
        down_low,
        down_high,
        up_columns >= down_high,
        up_columns,
        up_columns < up_high,
        slot_cap,
    )
    grad_hid_f = grad_local.astype(jnp.float32)
    grad_gate_pre = (grad_hid_f * up_pre * sigma * (1.0 + gate_pre * (1.0 - sigma))).astype(
        jnp.bfloat16
    )
    grad_up_pre = (grad_hid_f * gate_silu).astype(jnp.bfloat16)
    input_part = spread_back(
        w_gate, gate_blocks[:, 1], gate_blocks[:, 0], grad_gate_pre, block_rows
    )
    input_part = input_part + spread_back(
        w_up, up_blocks[:, 1], up_blocks[:, 0], grad_up_pre, block_rows
    )
    pair_pieces = block_grads(
        x_blocks,
        jnp.concatenate([gate_blocks[:, 0], up_blocks[:, 0]]),
        jnp.concatenate([grad_gate_pre, grad_up_pre], axis=0),
        jnp.concatenate([gate_blocks[:, 1], up_blocks[:, 1] + slot_cap]),
        token_norm,
    )
    width_all = block_rows * BS
    mp_count = lax.axis_size("mp")
    both_parts = jnp.stack(
        [
            branch_part.reshape(mp_count, width_all // mp_count, row_count).astype(jnp.bfloat16),
            input_part.reshape(mp_count, width_all // mp_count, row_count).astype(jnp.bfloat16),
        ],
        axis=1,
    )
    both_sums = lax.psum_scatter(
        both_parts.reshape(2 * width_all, row_count), "mp", scatter_dimension=0, tiled=True
    ).reshape(2, width_all // mp_count, row_count)
    branch_sum = both_sums[0].astype(jnp.float32)
    input_sum = both_sums[1].astype(jnp.float32)
    down_received = lax.all_to_all(down_groups, "dp", split_axis=0, concat_axis=0, tiled=True)
    down_total = jnp.sum(down_received, axis=0, dtype=jnp.float32)
    paired = pair_pieces.reshape(2, groups, -1, pair_pieces.shape[1])
    paired_received = lax.all_to_all(
        paired.transpose(1, 0, 2, 3), "dp", split_axis=0, concat_axis=0, tiled=True
    )
    paired_total = jnp.sum(paired_received, axis=0, dtype=jnp.float32)
    gate_total, up_total = paired_total[0], paired_total[1]
    return (
        branch_sum.astype(jnp.bfloat16),
        input_sum.astype(jnp.bfloat16),
        gate_total,
        up_total,
        down_total,
    )


def solution(mesh):
    in_specs = (
        P("mp", "dp"),
        P("mp", "dp"),
        P("mp", None),
        P("mp", None),
        P("mp", None),
        P("mp", None),
        P("mp", None),
        P("mp", None),
        P(),
        P(),
    )
    out_specs = (
        P("mp", "dp"),
        P("mp", "dp"),
        P(("mp", "dp"), None),
        P(("mp", "dp"), None),
        P(("mp", "dp"), None),
    )
    return jax.shard_map(local, mesh=mesh, in_specs=in_specs, out_specs=out_specs, check_vma=False)
```

```python
import math

import jax
import jax.numpy as jnp
from jax import lax
from jax.sharding import PartitionSpec as P

BS = 64
HC = 14


branch_scale = 1.0 / math.sqrt(80.0)


def shifted(value, axis, steps):
    count = lax.axis_size(axis)
    first, last = (max(0, -steps), min(count, count - steps))
    return lax.ppermute(value, axis, [(source, source + steps) for source in range(first, last)])


def segment_total(products, targets, out_count):
    choose = (targets[None, :] == jnp.arange(out_count, dtype=targets.dtype)[:, None]).astype(
        jnp.bfloat16
    )
    high = products.astype(jnp.bfloat16)
    low = (products - high.astype(jnp.float32)).astype(jnp.bfloat16)
    return jnp.einsum("sk,kor->sor", choose, high, preferred_element_type=jnp.float32) + jnp.einsum(
        "sk,kor->sor", choose, low, preferred_element_type=jnp.float32
    )


def spread_rows(weights, pick_rows, targets, source, out_count):
    blocks = weights.reshape(weights.shape[0], BS, BS)
    pieces = jnp.take(source, pick_rows, axis=0)
    products = jnp.einsum("kir,kio->kor", pieces, blocks, preferred_element_type=jnp.float32)
    return segment_total(products, targets, out_count)


def spread_back(weights, pick_rows, targets, source, out_count):
    blocks = weights.reshape(weights.shape[0], BS, BS)
    pieces = jnp.take(source, pick_rows, axis=0)
    products = jnp.einsum("kor,kio->kir", pieces, blocks, preferred_element_type=jnp.float32)
    return segment_total(products, targets, out_count)


def block_grads(left_side, left_rows, right_side, right_rows, factor):
    first_pick = jnp.take(left_side, left_rows, axis=0)
    second_pick = jnp.take(right_side, right_rows, axis=0)
    products = jnp.einsum(
        "kir,kor->kio", first_pick, second_pick, preferred_element_type=jnp.float32
    )
    return (products * factor).astype(jnp.bfloat16).reshape(products.shape[0], BS * BS)


def split_groups(pieces, groups):
    return pieces.reshape(groups, pieces.shape[0] // groups, pieces.shape[1])


def reduce_pieces(pieces, groups):
    received = lax.all_to_all(
        split_groups(pieces, groups), "dp", split_axis=0, concat_axis=0, tiled=True
    )
    return jnp.sum(received, axis=0, dtype=jnp.float32)


def pick_near(own, other, own_low, other_low, use_other, columns, filled, slot_cap):
    stacked = jnp.concatenate([own, other], axis=0)
    position = jnp.where(use_other, slot_cap + columns - other_low, columns - own_low)
    position = jnp.clip(jnp.where(filled, position, 0), 0, 2 * slot_cap - 1)
    picked = jnp.take(stacked, position, axis=0)
    return jnp.where(filled[:, None, None], picked, jnp.zeros_like(picked))


def local(
    x_feat,
    grad_out,
    w_gate,
    w_up,
    w_down,
    gate_blocks,
    up_blocks,
    down_blocks,
    up_offsets,
    down_offsets,
):
    row_count = x_feat.shape[1]
    slot_cap = HC + 3
    groups = lax.axis_size("dp")
    mp_index = lax.axis_index("mp")
    token_norm = 1.0 / math.sqrt(row_count * groups)
    both = lax.all_gather(jnp.stack([x_feat, grad_out]), "mp", axis=0, tiled=False)
    w_gate, w_up, w_down, both = lax.optimization_barrier(
        (w_gate.reshape(-1, BS, BS), w_up.reshape(-1, BS, BS), w_down.reshape(-1, BS, BS), both)
    )
    x_full = both[:, 0].reshape(-1, row_count)
    dy_full = both[:, 1].reshape(-1, row_count)
    block_rows = x_full.shape[0] // BS
    x_blocks = x_full.reshape(block_rows, BS, row_count)
    dy_blocks = dy_full.reshape(block_rows, BS, row_count)
    gate_pre = spread_rows(w_gate, gate_blocks[:, 0], gate_blocks[:, 1], x_blocks, slot_cap)
    up_pre = spread_rows(w_up, up_blocks[:, 0], up_blocks[:, 1], x_blocks, slot_cap)
    sigma = jax.nn.sigmoid(gate_pre)
    gate_silu = gate_pre * sigma
    hidden = (gate_silu * up_pre).astype(jnp.bfloat16)
    up_prev = jnp.take(up_offsets, jnp.maximum(mp_index - 1, 0))
    up_low = jnp.take(up_offsets, mp_index)
    up_high = jnp.take(up_offsets, mp_index + 1)
    down_low = jnp.take(down_offsets, mp_index)
    down_high = jnp.take(down_offsets, mp_index + 1)
    slot_range = jnp.arange(slot_cap, dtype=jnp.int32)
    lower_hidden = shifted(hidden, "mp", 1)
    down_columns = down_low + slot_range
    hidden_down = pick_near(
        hidden,
        lower_hidden,
        up_low,
        up_prev,
        down_columns < up_low,
        down_columns,
        down_columns < down_high,
        slot_cap,
    )
    branch_part = (
        spread_rows(w_down, down_blocks[:, 1], down_blocks[:, 0], hidden_down, block_rows)
        * branch_scale
    )
    down_piece = block_grads(
        hidden_down, down_blocks[:, 1], dy_blocks, down_blocks[:, 0], branch_scale * token_norm
    )
    down_groups, dy_late = lax.optimization_barrier((split_groups(down_piece, groups), dy_blocks))
    grad_hidden = (
        spread_back(w_down, down_blocks[:, 0], down_blocks[:, 1], dy_late, slot_cap)
        * branch_scale
    ).astype(jnp.bfloat16)
    upper_grad = shifted(grad_hidden, "mp", -1)
    up_columns = up_low + slot_range
    grad_local = pick_near(
        grad_hidden,
        upper_grad,
        down_low,
        down_high,
        up_columns >= down_high,
        up_columns,
        up_columns < up_high,
        slot_cap,
    )
    grad_hid_f = grad_local.astype(jnp.float32)
    grad_gate_pre = (grad_hid_f * up_pre * sigma * (1.0 + gate_pre * (1.0 - sigma))).astype(
        jnp.bfloat16
    )
    grad_up_pre = (grad_hid_f * gate_silu).astype(jnp.bfloat16)
    input_part = spread_back(
        w_gate, gate_blocks[:, 1], gate_blocks[:, 0], grad_gate_pre, block_rows
    )
    input_part = input_part + spread_back(
        w_up, up_blocks[:, 1], up_blocks[:, 0], grad_up_pre, block_rows
    )
    gate_piece = block_grads(
        x_blocks, gate_blocks[:, 0], grad_gate_pre, gate_blocks[:, 1], token_norm
    )
    up_piece = block_grads(x_blocks, up_blocks[:, 0], grad_up_pre, up_blocks[:, 1], token_norm)
    width_all = block_rows * BS
    mp_count = lax.axis_size("mp")
    both_parts = jnp.stack(
        [
            branch_part.reshape(mp_count, width_all // mp_count, row_count).astype(jnp.bfloat16),
            input_part.reshape(mp_count, width_all // mp_count, row_count).astype(jnp.bfloat16),
        ],
        axis=1,
    )
    both_sums = lax.psum_scatter(
        both_parts.reshape(2 * width_all, row_count), "mp", scatter_dimension=0, tiled=True
    ).reshape(2, width_all // mp_count, row_count)
    branch_sum = both_sums[0].astype(jnp.float32)
    input_sum = both_sums[1].astype(jnp.float32)
    down_received = lax.all_to_all(down_groups, "dp", split_axis=0, concat_axis=0, tiled=True)
    down_total = jnp.sum(down_received, axis=0, dtype=jnp.float32)
    paired = jnp.stack([gate_piece, up_piece]).reshape(2, groups, -1, gate_piece.shape[1])
    paired_received = lax.all_to_all(
        paired.transpose(1, 0, 2, 3), "dp", split_axis=0, concat_axis=0, tiled=True
    )
    paired_total = jnp.sum(paired_received, axis=0, dtype=jnp.float32)
    gate_total, up_total = paired_total[0], paired_total[1]
    return (
        branch_sum.astype(jnp.bfloat16),
        input_sum.astype(jnp.bfloat16),
        gate_total,
        up_total,
        down_total,
    )


def solution(mesh):
    in_specs = (
        P("mp", "dp"),
        P("mp", "dp"),
        P("mp", None),
        P("mp", None),
        P("mp", None),
        P("mp", None),
        P("mp", None),
        P("mp", None),
        P(),
        P(),
    )
    out_specs = (
        P("mp", "dp"),
        P("mp", "dp"),
        P(("mp", "dp"), None),
        P(("mp", "dp"), None),
        P(("mp", "dp"), None),
    )
    return jax.shard_map(local, mesh=mesh, in_specs=in_specs, out_specs=out_specs, check_vma=False)
```

```python
import math

import jax
import jax.numpy as jnp
from jax import lax
from jax.sharding import PartitionSpec as P

BS = 64
HC = 14


branch_scale = 1.0 / math.sqrt(80.0)


def shifted(value, axis, steps):
    count = lax.axis_size(axis)
    first, last = (max(0, -steps), min(count, count - steps))
    return lax.ppermute(value, axis, [(source, source + steps) for source in range(first, last)])


def segment_total(products, targets, out_count):
    choose = (targets[None, :] == jnp.arange(out_count, dtype=targets.dtype)[:, None]).astype(jnp.float32)
    return jnp.einsum(
        "sk,kor->sor",
        choose,
        products,
        precision=lax.Precision.DEFAULT,
        preferred_element_type=jnp.float32,
    )


def spread_rows(weights, pick_rows, targets, source, out_count):
    blocks = weights.reshape(weights.shape[0], BS, BS)
    pieces = jnp.take(source, pick_rows, axis=0)
    products = jnp.einsum("kir,kio->kor", pieces, blocks, preferred_element_type=jnp.float32)
    return segment_total(products, targets, out_count)


def spread_back(weights, pick_rows, targets, source, out_count):
    blocks = weights.reshape(weights.shape[0], BS, BS)
    pieces = jnp.take(source, pick_rows, axis=0)
    products = jnp.einsum("kor,kio->kir", pieces, blocks, preferred_element_type=jnp.float32)
    return segment_total(products, targets, out_count)


def block_grads(left_side, left_rows, right_side, right_rows, factor):
    first_pick = jnp.take(left_side, left_rows, axis=0)
    second_pick = jnp.take(right_side, right_rows, axis=0)
    products = jnp.einsum(
        "kir,kor->kio", first_pick, second_pick, preferred_element_type=jnp.float32
    )
    return (products * factor).astype(jnp.bfloat16).reshape(products.shape[0], BS * BS)


def split_groups(pieces, groups):
    return pieces.reshape(groups, pieces.shape[0] // groups, pieces.shape[1])


def reduce_pieces(pieces, groups):
    received = lax.all_to_all(
        split_groups(pieces, groups), "dp", split_axis=0, concat_axis=0, tiled=True
    )
    return jnp.sum(received, axis=0, dtype=jnp.float32)


def pick_near(own, other, own_low, other_low, use_other, columns, filled, slot_cap):
    stacked = jnp.concatenate([own, other], axis=0)
    position = jnp.where(use_other, slot_cap + columns - other_low, columns - own_low)
    position = jnp.clip(jnp.where(filled, position, 0), 0, 2 * slot_cap - 1)
    picked = jnp.take(stacked, position, axis=0)
    return jnp.where(filled[:, None, None], picked, jnp.zeros_like(picked))


def local(
    x_feat,
    grad_out,
    w_gate,
    w_up,
    w_down,
    gate_blocks,
    up_blocks,
    down_blocks,
    up_offsets,
    down_offsets,
):
    row_count = x_feat.shape[1]
    slot_cap = HC + 3
    groups = lax.axis_size("dp")
    mp_index = lax.axis_index("mp")
    token_norm = 1.0 / math.sqrt(row_count * groups)
    both = lax.all_gather(jnp.stack([x_feat, grad_out]), "mp", axis=0, tiled=False)
    w_gate, w_up, w_down, both = lax.optimization_barrier(
        (w_gate.reshape(-1, BS, BS), w_up.reshape(-1, BS, BS), w_down.reshape(-1, BS, BS), both)
    )
    x_full = both[:, 0].reshape(-1, row_count)
    dy_full = both[:, 1].reshape(-1, row_count)
    block_rows = x_full.shape[0] // BS
    x_blocks = x_full.reshape(block_rows, BS, row_count)
    dy_blocks = dy_full.reshape(block_rows, BS, row_count)
    gate_pre = spread_rows(w_gate, gate_blocks[:, 0], gate_blocks[:, 1], x_blocks, slot_cap)
    up_pre = spread_rows(w_up, up_blocks[:, 0], up_blocks[:, 1], x_blocks, slot_cap)
    sigma = jax.nn.sigmoid(gate_pre)
    gate_silu = gate_pre * sigma
    hidden = (gate_silu * up_pre).astype(jnp.bfloat16)
    up_prev = jnp.take(up_offsets, jnp.maximum(mp_index - 1, 0))
    up_low = jnp.take(up_offsets, mp_index)
    up_high = jnp.take(up_offsets, mp_index + 1)
    down_low = jnp.take(down_offsets, mp_index)
    down_high = jnp.take(down_offsets, mp_index + 1)
    slot_range = jnp.arange(slot_cap, dtype=jnp.int32)
    lower_hidden = shifted(hidden, "mp", 1)
    down_columns = down_low + slot_range
    hidden_down = pick_near(
        hidden,
        lower_hidden,
        up_low,
        up_prev,
        down_columns < up_low,
        down_columns,
        down_columns < down_high,
        slot_cap,
    )
    branch_part = (
        spread_rows(w_down, down_blocks[:, 1], down_blocks[:, 0], hidden_down, block_rows)
        * branch_scale
    )
    down_piece = block_grads(
        hidden_down, down_blocks[:, 1], dy_blocks, down_blocks[:, 0], branch_scale * token_norm
    )
    down_groups, dy_late = lax.optimization_barrier((split_groups(down_piece, groups), dy_blocks))
    grad_hidden = (
        spread_back(w_down, down_blocks[:, 0], down_blocks[:, 1], dy_late, slot_cap)
        * branch_scale
    ).astype(jnp.bfloat16)
    upper_grad = shifted(grad_hidden, "mp", -1)
    up_columns = up_low + slot_range
    grad_local = pick_near(
        grad_hidden,
        upper_grad,
        down_low,
        down_high,
        up_columns >= down_high,
        up_columns,
        up_columns < up_high,
        slot_cap,
    )
    grad_hid_f = grad_local.astype(jnp.float32)
    grad_gate_pre = (grad_hid_f * up_pre * sigma * (1.0 + gate_pre * (1.0 - sigma))).astype(
        jnp.bfloat16
    )
    grad_up_pre = (grad_hid_f * gate_silu).astype(jnp.bfloat16)
    input_part = spread_back(
        w_gate, gate_blocks[:, 1], gate_blocks[:, 0], grad_gate_pre, block_rows
    )
    input_part = input_part + spread_back(
        w_up, up_blocks[:, 1], up_blocks[:, 0], grad_up_pre, block_rows
    )
    gate_piece = block_grads(
        x_blocks, gate_blocks[:, 0], grad_gate_pre, gate_blocks[:, 1], token_norm
    )
    up_piece = block_grads(x_blocks, up_blocks[:, 0], grad_up_pre, up_blocks[:, 1], token_norm)
    width_all = block_rows * BS
    mp_count = lax.axis_size("mp")
    both_parts = jnp.stack(
        [
            branch_part.reshape(mp_count, width_all // mp_count, row_count).astype(jnp.bfloat16),
            input_part.reshape(mp_count, width_all // mp_count, row_count).astype(jnp.bfloat16),
        ],
        axis=1,
    )
    both_sums = lax.psum_scatter(
        both_parts.reshape(2 * width_all, row_count), "mp", scatter_dimension=0, tiled=True
    ).reshape(2, width_all // mp_count, row_count)
    branch_sum = both_sums[0].astype(jnp.float32)
    input_sum = both_sums[1].astype(jnp.float32)
    down_received = lax.all_to_all(down_groups, "dp", split_axis=0, concat_axis=0, tiled=True)
    down_total = jnp.sum(down_received, axis=0, dtype=jnp.float32)
    paired = jnp.stack([gate_piece, up_piece]).reshape(2, groups, -1, gate_piece.shape[1])
    paired_received = lax.all_to_all(
        paired.transpose(1, 0, 2, 3), "dp", split_axis=0, concat_axis=0, tiled=True
    )
    paired_total = jnp.sum(paired_received, axis=0, dtype=jnp.float32)
    gate_total, up_total = paired_total[0], paired_total[1]
    return (
        branch_sum.astype(jnp.bfloat16),
        input_sum.astype(jnp.bfloat16),
        gate_total,
        up_total,
        down_total,
    )


def solution(mesh):
    in_specs = (
        P("mp", "dp"),
        P("mp", "dp"),
        P("mp", None),
        P("mp", None),
        P("mp", None),
        P("mp", None),
        P("mp", None),
        P("mp", None),
        P(),
        P(),
    )
    out_specs = (
        P("mp", "dp"),
        P("mp", "dp"),
        P(("mp", "dp"), None),
        P(("mp", "dp"), None),
        P(("mp", "dp"), None),
    )
    return jax.shard_map(local, mesh=mesh, in_specs=in_specs, out_specs=out_specs, check_vma=False)
```
